128 devices in a mesh: lat: 32 (over z, y, core), chan: 4 (over x).
Axes of the slice: x: 4, y: 4, z: 4, core: 2. Of those that a mesh axis runs over, the one named last changes fastest.
Arguments:
- field: bfloat16 [32, 3, 2, 512, 4096], P('chan', None, None, 'lat'), may hold values from -6 to 6
- mix_weight: bfloat16 [32, 32], replicated, may hold values from -1 to 1
- spectral_gain: float32 [32, 2048], P('chan'), may hold values from 0.05 to 1
- legendre: bfloat16 [2, 512, 512, 1024], P(None, 'lat'), may hold values from -0.25 to 0.25
- slot_mode: int32 [512], replicated, may hold values from 0 to 511, as said below
Outputs:
- layered: bfloat16 [32, 3, 2, 512, 4096], P('chan', None, None, 'lat')
The draws below stay inside these ranges and needn't reach their ends.
Inputs may be any that keep to these rules, and one draw needn't show every extreme that they name: `slot_mode`: A permutation of the mode indices; slots 2 j and 2 j + 1 carry the modes k and 511 - k for some k, so the slots of every index of lat carry whole such pairs.
All inputs are finite; a program needn't handle non-finite values.
Results may differ from the reference program's by a relative error of at most 0.0085.
Values may be sent and summed in bfloat16 or wider, within the bound.
No kernel may reach another device: no remote copies, remote signals or barrier semaphores. Data moves between devices by JAX's collectives and lax.ppermute only.
A program may use at most 192 MiB of HBM per device.

```python
import math
import jax
import jax.numpy as jnp
from jax import lax

CH = 32
LMAX = 2048
TAN = 3
LH = 1024
NPHI = 4096
M = 512
MSTEP = 4
NRN = 512


def draw_slot_mode(key, part):
    pair_count = M // 2
    pair_order = jax.random.permutation(jax.random.fold_in(key, 11), pair_count)
    flips = jax.random.randint(jax.random.fold_in(key, 12), (pair_count,), 0, 2)
    first_mode = jnp.where(flips == 1, pair_order, M - 1 - pair_order)
    second_mode = M - 1 - first_mode
    return jnp.stack([first_mode, second_mode], axis=1).reshape(M).astype(jnp.int32)


def level_of(key, extent, pieces, least, top_value):
    loudness = 1.0
    for dim, blocks in pieces:
        draws = jax.random.uniform(jax.random.fold_in(jax.random.fold_in(key, 6), dim), (blocks,), jnp.float32, least / len(pieces), top_value / len(pieces))
        loudness = loudness * jnp.repeat(jnp.exp(draws), extent[dim] // blocks).reshape((-1,) + (1,) * (len(extent) - 1 - dim))
    return loudness


def gaussian(own_key, extent, spread, reach, pieces=(), kind=jnp.bfloat16):
    factor_of = level_of(own_key, extent, pieces, -0.22, 0.18) if pieces else 1.0
    values = jax.random.normal(own_key, extent, jnp.float32) * spread * factor_of
    return jnp.minimum(jnp.maximum(values, -reach), reach).astype(kind)


def setup_inputs(seed: int = 0) -> dict:
    keys = jax.random.split(jax.random.key(seed), 6)
    return {
        "field": gaussian(keys[0], (CH, TAN, 2, NRN, NPHI), 1.0, 6.0, ((0, 4), (3, 32))),
        "mix_weight": gaussian(keys[1], (CH, CH), CH ** -0.5, 1.0),
        "spectral_gain": jnp.clip(jnp.exp(math.log(1.0) - 2.9957323 * jax.random.uniform(keys[2], (CH, LMAX), jnp.float32) ** level_of(keys[2], (CH, LMAX), ((0, 4),), -0.2, 0.2)), 0.05, 1.0),
        "legendre": gaussian(keys[3], (2, M, NRN, LH), NRN ** -0.5, 0.25, ((1, 32),)),
        "slot_mode": draw_slot_mode(jax.random.fold_in(keys[5], 71), 0),
    }


def reference(field, mix_weight, spectral_gain, legendre, slot_mode):
    mode_values = (slot_mode * MSTEP).astype(jnp.int32)
    places = jnp.arange(NPHI, dtype=jnp.int32)
    turns = places[:, None] * mode_values[None, :] % NPHI
    angles = turns.astype(jnp.float32) * (2.0 * math.pi / NPHI)
    basis = jnp.concatenate([jnp.cos(angles), -jnp.sin(angles)], axis=1)
    forward_table = (basis * math.sqrt(2.0 / NPHI)).astype(jnp.bfloat16)
    inverse_table = (basis.T * math.sqrt(1.0 / M)).astype(jnp.bfloat16)

    def forward(channel_block):
        rows = channel_block.reshape(-1, NPHI)
        spectra = jnp.dot(rows, forward_table, preferred_element_type=jnp.float32)
        return spectra.astype(jnp.bfloat16).reshape(TAN, 2, NRN, 2, M)
    spectrum = lax.map(forward, field)
    mixed_spec = jnp.einsum('oc,cthrqs->othrqs', mix_weight.astype(jnp.float32), spectrum.astype(jnp.float32))
    even_sum = mixed_spec[:, :, 0] + mixed_spec[:, :, 1]
    odd_sum = mixed_spec[:, :, 0] - mixed_spec[:, :, 1]
    folded = jnp.stack([even_sum, odd_sum], axis=2).astype(jnp.bfloat16)
    by_slot = jnp.moveaxis(folded, -1, 0)
    slot_tables = jnp.moveaxis(legendre, 1, 0)
    gain_par = jnp.transpose(spectral_gain.reshape(CH, LH, 2), (0, 2, 1))[:, None, :, None, :]
    degree = 2 * jnp.arange(LH, dtype=jnp.int32)[None, :] + jnp.arange(2, dtype=jnp.int32)[:, None]

    def per_slot(bundle):
        leg_table, slot_block, mode_value = bundle
        leg_table = leg_table.astype(jnp.float32)
        coefficients = jnp.einsum('ctprq,pri->ctpqi', slot_block.astype(jnp.float32), leg_table)
        allowed = (degree >= mode_value)[None, None, :, None, :]
        filtered = jnp.where(allowed, gain_par * coefficients, 0.0).astype(jnp.bfloat16)
        synthesis = jnp.einsum('ctpqi,pri->ctprq', filtered.astype(jnp.float32), leg_table)
        northern = synthesis[:, :, 0] + synthesis[:, :, 1]
        southern = synthesis[:, :, 0] - synthesis[:, :, 1]
        return jnp.stack([northern, southern], axis=2).astype(jnp.bfloat16)
    returned = lax.map(per_slot, (slot_tables, by_slot, mode_values))
    returned = jnp.moveaxis(returned, 0, -1)

    def inverse(bundle):
        spectra, initial = bundle
        rows = spectra.reshape(-1, 2 * M)
        waveform = jnp.dot(rows, inverse_table, preferred_element_type=jnp.float32).reshape(TAN, 2, NRN, NPHI)
        primal_h = waveform[0]
        sigmoid_h = jax.nn.sigmoid(primal_h)
        slope_h = sigmoid_h * (1.0 + primal_h * (1.0 - sigmoid_h))
        initial_f = initial.astype(jnp.float32)
        primal = initial_f[0] + primal_h * sigmoid_h
        tangents = initial_f[1:] + slope_h[None] * waveform[1:]
        return jnp.concatenate([primal[None], tangents], axis=0).astype(jnp.bfloat16)
    return lax.map(inverse, (returned, field))
```

```python
import math

import jax
import jax.numpy as jnp
from jax import lax
from jax.sharding import PartitionSpec as P


def trig_tables(modes, period, points):
    inner = 1 << ((period.bit_length() - 1) // 2)
    outer = period // inner
    scale = 2.0 * math.pi / points
    hi_turns = (lax.iota(jnp.int32, outer)[None, :] * inner * modes[:, None]) % points
    lo_turns = (lax.iota(jnp.int32, inner)[None, :] * modes[:, None]) % points
    hi_angle = hi_turns.astype(jnp.float32) * scale
    lo_angle = lo_turns.astype(jnp.float32) * scale
    ca, sa = jnp.cos(hi_angle)[:, :, None], jnp.sin(hi_angle)[:, :, None]
    cb, sb = jnp.cos(lo_angle)[:, None, :], jnp.sin(lo_angle)[:, None, :]
    cosine = (ca * cb - sa * sb).reshape(modes.shape[0], period)
    sine = (sa * cb + ca * sb).reshape(modes.shape[0], period)
    return cosine, sine


def local(field, mix_weight, spectral_gain, legendre, slot_mode, n_lat, n_chan):
    chans = field.shape[0]
    fields = field.shape[1]
    cycles = field.shape[3]
    points = field.shape[4]
    total_modes = slot_mode.shape[0]
    degrees = spectral_gain.shape[1]
    half_deg = degrees // 2
    step_size = degrees // total_modes
    period = points // math.gcd(points, step_size)
    devices = n_lat * n_chan
    per_dev = total_modes // devices
    north = legendre.shape[2]
    lat_index = lax.axis_index("lat")
    chan_index = lax.axis_index("chan")
    me = lat_index * n_chan + chan_index

    modes = slot_mode * step_size
    cosine, sine = trig_tables(modes, period, points)
    basis = jnp.concatenate(
        [cosine.reshape(devices, 1, per_dev, period), -sine.reshape(devices, 1, per_dev, period)],
        axis=1,
    ).reshape(2 * total_modes, period)
    fwd = (basis * math.sqrt(2.0 / points)).astype(jnp.bfloat16)
    inv = (basis * math.sqrt(1.0 / total_modes)).astype(jnp.bfloat16)

    wide = field.astype(jnp.float32).reshape(chans, fields, 2, cycles, points // period, period)
    summed = wide.sum(axis=4)
    high = summed.astype(jnp.bfloat16)
    low = (summed - high.astype(jnp.float32)).astype(jnp.bfloat16)
    rows = jnp.concatenate([high, low], axis=-1).reshape(-1, 2 * period)
    spec_t = lax.dot_general(
        jnp.concatenate([fwd, fwd], axis=1), rows, (((1,), (1,)), ((), ())),
        preferred_element_type=jnp.float32,
    ).astype(jnp.bfloat16)
    row_count = rows.shape[0]

    sent = spec_t.reshape(devices, 2 * per_dev, row_count)
    got = lax.all_to_all(sent, ("lat", "chan"), 0, 0, tiled=True)
    got = got.reshape(n_lat, n_chan, 2, per_dev, chans, fields, 2, cycles)
    weight = mix_weight.reshape(-1, n_chan, chans)
    mixed = jnp.einsum(
        "oCk,LCqsktHr->sHqtoLr", weight, got, preferred_element_type=jnp.float32
    )
    mixed = mixed.reshape(per_dev, 2, 2, fields, -1, north)
    folded = jnp.stack(
        [mixed[:, 0] + mixed[:, 1], mixed[:, 0] - mixed[:, 1]], axis=1
    ).astype(jnp.bfloat16)
    folded = folded.reshape(per_dev, 2, -1, north)

    leg = lax.dynamic_slice_in_dim(legendre, chan_index * per_dev, per_dev, 1)
    coefficients = jnp.einsum(
        "spxr,psri->spxi", folded, leg, preferred_element_type=jnp.float32
    )
    all_gain = lax.all_gather(spectral_gain, "chan", axis=0, tiled=True)
    gain_par = jnp.transpose(all_gain.reshape(-1, half_deg, 2), (2, 0, 1))
    own_modes = lax.dynamic_slice_in_dim(modes, me * per_dev, per_dev, 0)
    degree = 2 * lax.iota(jnp.int32, half_deg)[None, :] + lax.iota(jnp.int32, 2)[:, None]
    allowed = degree[None, :, :] >= own_modes[:, None, None]
    coefficients = coefficients.reshape(per_dev, 2, 2, fields, -1, half_deg)
    filtered = jnp.where(
        allowed[:, :, None, None, None, :],
        gain_par[None, :, None, None, :, :] * coefficients,
        0.0,
    ).astype(jnp.bfloat16)
    filtered = filtered.reshape(per_dev, 2, -1, half_deg)
    synthesis = jnp.einsum(
        "spxi,psri->spxr", filtered, leg, preferred_element_type=jnp.float32
    )
    back = jnp.stack(
        [synthesis[:, 0] + synthesis[:, 1], synthesis[:, 0] - synthesis[:, 1]], axis=1
    ).astype(jnp.bfloat16)
    back = back.reshape(per_dev, 2, 2, fields, n_chan, chans, n_lat, cycles)
    leaving = jnp.transpose(back, (6, 4, 2, 0, 5, 3, 1, 7)).reshape(devices, 2 * per_dev, row_count)
    returned = lax.all_to_all(leaving, ("lat", "chan"), 0, 0, tiled=True)
    returned = returned.reshape(2 * total_modes, row_count)

    waveform = lax.dot_general(
        returned, inv, (((0,), (0,)), ((), ())), preferred_element_type=jnp.float32
    )
    waveform = waveform.reshape(chans, fields, 2, cycles, 1, period)
    primal_h = waveform[:, 0]
    sigmoid_h = jax.nn.sigmoid(primal_h)
    slope_h = sigmoid_h * (1.0 + primal_h * (1.0 - sigmoid_h))
    initial = field.astype(jnp.float32).reshape(chans, fields, 2, cycles, points // period, period)
    primal = initial[:, 0] + primal_h * sigmoid_h
    tangents = initial[:, 1:] + slope_h[:, None] * waveform[:, 1:]
    out = jnp.concatenate([primal[:, None], tangents], axis=1).astype(jnp.bfloat16)
    return out.reshape(field.shape)


def solution(mesh):
    n_lat = mesh.shape["lat"]
    n_chan = mesh.shape["chan"]
    placed = (
        P("chan", None, None, "lat", None),
        P(),
        P("chan", None),
        P(None, "lat", None, None),
        P(),
    )

    def body(field, mix_weight, spectral_gain, legendre, slot_mode):
        return local(field, mix_weight, spectral_gain, legendre, slot_mode, n_lat, n_chan)

    return jax.shard_map(
        body,
        mesh=mesh,
        in_specs=placed,
        out_specs=P("chan", None, None, "lat", None),
        check_vma=False,
    )
```

```python
import math

import jax
import jax.numpy as jnp
from jax import lax
from jax.sharding import PartitionSpec as P


def trig_tables(modes, period, points):
    lanes = min(128, period)
    blocks = period // lanes
    scale = 2.0 * math.pi / points
    hi_turns = (lax.iota(jnp.int32, blocks)[None, :] * lanes * modes[:, None]) % points
    lo_turns = (lax.iota(jnp.int32, lanes)[None, :] * modes[:, None]) % points
    hi_angle = hi_turns.astype(jnp.float32) * scale
    lo_angle = lo_turns.astype(jnp.float32) * scale
    ca, sa = jnp.cos(hi_angle), jnp.sin(hi_angle)
    cb, sb = jnp.cos(lo_angle), jnp.sin(lo_angle)
    cosine = jnp.concatenate(
        [ca[:, a : a + 1] * cb - sa[:, a : a + 1] * sb for a in range(blocks)], axis=1
    )
    sine = jnp.concatenate(
        [sa[:, a : a + 1] * cb + ca[:, a : a + 1] * sb for a in range(blocks)], axis=1
    )
    return cosine, sine


def local(field, mix_weight, spectral_gain, legendre, slot_mode, n_lat, n_chan):
    chans = field.shape[0]
    fields = field.shape[1]
    cycles = field.shape[3]
    points = field.shape[4]
    total_modes = slot_mode.shape[0]
    degrees = spectral_gain.shape[1]
    half_deg = degrees // 2
    step_size = degrees // total_modes
    period = points // math.gcd(points, step_size)
    devices = n_lat * n_chan
    per_dev = total_modes // devices
    north = legendre.shape[2]
    lat_index = lax.axis_index("lat")
    chan_index = lax.axis_index("chan")
    me = lat_index * n_chan + chan_index

    modes = slot_mode * step_size
    cosine, sine = trig_tables(modes, period, points)
    basis = jnp.concatenate(
        [cosine.reshape(devices, 1, per_dev, period), -sine.reshape(devices, 1, per_dev, period)],
        axis=1,
    ).reshape(2 * total_modes, period)
    fwd = (basis * math.sqrt(2.0 / points)).astype(jnp.bfloat16)
    inv = (basis * math.sqrt(1.0 / total_modes)).astype(jnp.bfloat16)

    flat = field.reshape(-1, points)
    summed = flat[:, :period].astype(jnp.float32)
    for n in range(1, points // period):
        summed = summed + flat[:, n * period : (n + 1) * period].astype(jnp.float32)
    high = summed.astype(jnp.bfloat16)
    low = (summed - high.astype(jnp.float32)).astype(jnp.bfloat16)
    rows = jnp.concatenate([high, low], axis=1)
    spec_t = lax.dot_general(
        jnp.concatenate([fwd, fwd], axis=1), rows, (((1,), (1,)), ((), ())),
        preferred_element_type=jnp.float32,
    ).astype(jnp.bfloat16)
    row_count = rows.shape[0]

    sent = spec_t.reshape(devices, 2 * per_dev, row_count)
    got = lax.all_to_all(sent, ("lat", "chan"), 0, 0, tiled=True)
    got = got.reshape(n_lat, n_chan, 2, per_dev, chans, fields, 2, cycles)
    weight = mix_weight.reshape(-1, n_chan, chans)
    mixed = jnp.einsum(
        "oCk,LCqsktHr->sHqtoLr", weight, got, preferred_element_type=jnp.float32
    )
    mixed = mixed.reshape(per_dev, 2, 2, fields, -1, north)
    folded = jnp.stack(
        [mixed[:, 0] + mixed[:, 1], mixed[:, 0] - mixed[:, 1]], axis=1
    ).astype(jnp.bfloat16)
    folded = folded.reshape(per_dev, 2, -1, north)

    leg = lax.dynamic_slice_in_dim(legendre, chan_index * per_dev, per_dev, 1)
    coefficients = jnp.einsum(
        "spxr,psri->spxi", folded, leg, preferred_element_type=jnp.float32
    )
    all_gain = lax.all_gather(spectral_gain, "chan", axis=0, tiled=True)
    gain_par = jnp.transpose(all_gain.reshape(-1, half_deg, 2), (2, 0, 1))
    own_modes = lax.dynamic_slice_in_dim(modes, me * per_dev, per_dev, 0)
    degree = 2 * lax.iota(jnp.int32, half_deg)[None, :] + lax.iota(jnp.int32, 2)[:, None]
    allowed = degree[None, :, :] >= own_modes[:, None, None]
    coefficients = coefficients.reshape(per_dev, 2, 2, fields, -1, half_deg)
    filtered = jnp.where(
        allowed[:, :, None, None, None, :],
        gain_par[None, :, None, None, :, :] * coefficients,
        0.0,
    ).astype(jnp.bfloat16)
    filtered = filtered.reshape(per_dev, 2, -1, half_deg)
    synthesis = jnp.einsum(
        "spxi,psri->spxr", filtered, leg, preferred_element_type=jnp.float32
    )
    back = jnp.stack(
        [synthesis[:, 0] + synthesis[:, 1], synthesis[:, 0] - synthesis[:, 1]], axis=1
    ).astype(jnp.bfloat16)
    back = back.reshape(per_dev, 2, 2, fields, n_chan, chans, n_lat, cycles)
    leaving = jnp.transpose(back, (6, 4, 2, 0, 5, 3, 1, 7)).reshape(devices, 2 * per_dev, row_count)
    returned = lax.all_to_all(leaving, ("lat", "chan"), 0, 0, tiled=True)
    returned = returned.reshape(2 * total_modes, row_count)

    waveform = lax.dot_general(
        returned, inv, (((0,), (0,)), ((), ())), preferred_element_type=jnp.float32
    )
    waveform = waveform.reshape(chans, fields, -1, period)
    primal_h = waveform[:, 0]
    sigmoid_h = jax.nn.sigmoid(primal_h)
    slope_h = sigmoid_h * (1.0 + primal_h * (1.0 - sigmoid_h))
    gain_h = primal_h * sigmoid_h
    flat = field.reshape(chans, fields, -1, points)
    pieces = []
    for n in range(points // period):
        initial = flat[:, :, :, n * period : (n + 1) * period].astype(jnp.float32)
        primal = initial[:, 0] + gain_h
        tangents = initial[:, 1:] + slope_h[:, None] * waveform[:, 1:]
        pieces.append(jnp.concatenate([primal[:, None], tangents], axis=1).astype(jnp.bfloat16))
    out = jnp.concatenate(pieces, axis=3)
    return out.reshape(field.shape)


def solution(mesh):
    n_lat = mesh.shape["lat"]
    n_chan = mesh.shape["chan"]
    placed = (
        P("chan", None, None, "lat", None),
        P(),
        P("chan", None),
        P(None, "lat", None, None),
        P(),
    )

    def body(field, mix_weight, spectral_gain, legendre, slot_mode):
        return local(field, mix_weight, spectral_gain, legendre, slot_mode, n_lat, n_chan)

    return jax.shard_map(
        body,
        mesh=mesh,
        in_specs=placed,
        out_specs=P("chan", None, None, "lat", None),
        check_vma=False,
    )
```

```python
import math

import jax
import jax.numpy as jnp
from jax import lax
from jax.sharding import PartitionSpec as P


def local(field, mix_weight, spectral_gain, legendre, slot_mode, n_lat, n_chan):
    chans = field.shape[0]
    fields = field.shape[1]
    cycles = field.shape[3]
    points = field.shape[4]
    total_modes = slot_mode.shape[0]
    degrees = spectral_gain.shape[1]
    half_deg = degrees // 2
    step_size = degrees // total_modes
    period = points // math.gcd(points, step_size)
    devices = n_lat * n_chan
    per_dev = total_modes // devices
    lat_index = lax.axis_index("lat")
    chan_index = lax.axis_index("chan")
    row_count = chans * fields * 2 * cycles

    modes = (slot_mode * step_size).reshape(n_lat, n_chan, per_dev)
    modes = jnp.transpose(modes, (1, 0, 2)).reshape(devices, 1, per_dev)
    quarter = jnp.array([0, points // 4], jnp.int32).reshape(1, 2, 1)
    places = lax.iota(jnp.int32, period)
    turns = (modes[..., None] * places + quarter[..., None]) % points
    basis = jnp.cos(turns.astype(jnp.float32) * (2.0 * math.pi / points)).reshape(-1, period)
    fwd = (basis * math.sqrt(2.0 / points)).astype(jnp.bfloat16)
    inv = (basis * math.sqrt(1.0 / total_modes)).astype(jnp.bfloat16)

    flat = field.reshape(-1, points)
    summed = flat[:, :period].astype(jnp.float32)
    for n in range(1, points // period):
        summed = summed + flat[:, n * period : (n + 1) * period].astype(jnp.float32)
    high = summed.astype(jnp.bfloat16)
    low = (summed - high.astype(jnp.float32)).astype(jnp.bfloat16)
    rows = jnp.concatenate([high, low], axis=1)
    spec_t = lax.dot_general(
        jnp.concatenate([fwd, fwd], axis=1), rows, (((1,), (1,)), ((), ())),
        preferred_element_type=jnp.float32,
    ).astype(jnp.bfloat16)

    sent = spec_t.reshape(devices, 2, per_dev, chans, fields, 2, cycles)
    got = lax.all_to_all(sent, ("chan", "lat"), 0, 6, tiled=True)
    got = got.reshape(2, per_dev, chans, fields, 2, n_chan, n_lat * cycles)
    sign = jnp.array([[1.0, 1.0], [1.0, -1.0]], jnp.float32)
    weight = mix_weight.astype(jnp.float32).reshape(-1, n_chan, chans)
    mix_fold = (sign[:, None, None, :, None] * jnp.transpose(weight, (0, 2, 1))[None, :, :, None, :])
    mix_fold = mix_fold.astype(jnp.bfloat16)
    folded = jnp.einsum(
        "pokhC,qskthCr->sptqor", mix_fold, got, preferred_element_type=jnp.float32
    ).astype(jnp.bfloat16)

    leg = lax.dynamic_slice_in_dim(legendre, chan_index * per_dev, per_dev, 1)
    coefficients = jnp.einsum(
        "sptqor,psri->sptqoi", folded, leg, preferred_element_type=jnp.float32
    )
    all_gain = lax.all_gather(spectral_gain, "chan", axis=0, tiled=True)
    gain_par = jnp.transpose(all_gain.reshape(-1, half_deg, 2), (2, 0, 1))
    own_modes = lax.dynamic_slice_in_dim(
        modes.reshape(-1), (chan_index * n_lat + lat_index) * per_dev, per_dev, 0
    )
    degree = 2 * lax.iota(jnp.int32, half_deg)[None, :] + lax.iota(jnp.int32, 2)[:, None]
    allowed = degree[None, :, :] >= own_modes[:, None, None]
    filtered = jnp.where(
        allowed[:, :, None, None, None, :],
        gain_par[None, :, None, None, :, :] * coefficients,
        0.0,
    ).astype(jnp.bfloat16)
    synthesis = jnp.einsum(
        "sptqoi,psri->sptqor", filtered, leg, preferred_element_type=jnp.float32
    )
    back = jnp.stack(
        [synthesis[:, 0] + synthesis[:, 1], synthesis[:, 0] - synthesis[:, 1]], axis=1
    ).astype(jnp.bfloat16)
    back = back.reshape(per_dev, 2, fields, 2, n_chan, chans, n_lat, cycles)
    leaving = jnp.transpose(back, (4, 6, 3, 0, 5, 2, 1, 7)).reshape(devices, 2 * per_dev, row_count)
    returned = lax.all_to_all(leaving, ("chan", "lat"), 0, 0, tiled=True)
    returned = returned.reshape(2 * total_modes, row_count)

    waveform = lax.dot_general(
        returned, inv, (((0,), (0,)), ((), ())), preferred_element_type=jnp.float32
    )
    waveform = waveform.reshape(chans, fields, -1, period)
    primal_h = waveform[:, 0]
    sigmoid_h = jax.nn.sigmoid(primal_h)
    slope_h = sigmoid_h * (1.0 + primal_h * (1.0 - sigmoid_h))
    gain_h = primal_h * sigmoid_h
    flat = field.reshape(chans, fields, -1, points)
    pieces = []
    for n in range(points // period):
        initial = flat[:, :, :, n * period : (n + 1) * period].astype(jnp.float32)
        primal = initial[:, 0] + gain_h
        tangents = initial[:, 1:] + slope_h[:, None] * waveform[:, 1:]
        pieces.append(jnp.concatenate([primal[:, None], tangents], axis=1).astype(jnp.bfloat16))
    out = jnp.concatenate(pieces, axis=3)
    return out.reshape(field.shape)


def solution(mesh):
    n_lat = mesh.shape["lat"]
    n_chan = mesh.shape["chan"]
    placed = (
        P("chan", None, None, "lat", None),
        P(),
        P("chan", None),
        P(None, "lat", None, None),
        P(),
    )

    def body(field, mix_weight, spectral_gain, legendre, slot_mode):
        return local(field, mix_weight, spectral_gain, legendre, slot_mode, n_lat, n_chan)

    return jax.shard_map(
        body,
        mesh=mesh,
        in_specs=placed,
        out_specs=P("chan", None, None, "lat", None),
        check_vma=False,
    )
```

```python
import math

import jax
import jax.numpy as jnp
from jax import lax
from jax.sharding import PartitionSpec as P


def local(field, mix_weight, spectral_gain, legendre, slot_mode, n_lat, n_chan):
    chans = field.shape[0]
    fields = field.shape[1]
    cycles = field.shape[3]
    points = field.shape[4]
    total_modes = slot_mode.shape[0]
    degrees = spectral_gain.shape[1]
    half_deg = degrees // 2
    step_size = degrees // total_modes
    period = points // math.gcd(points, step_size)
    devices = n_lat * n_chan
    per_dev = total_modes // devices
    lat_index = lax.axis_index("lat")
    chan_index = lax.axis_index("chan")
    row_count = chans * fields * 2 * cycles

    modes = (slot_mode * step_size).reshape(n_lat, n_chan, per_dev)
    modes = jnp.transpose(modes, (1, 0, 2)).reshape(devices, 1, per_dev)
    quarter = jnp.array([0, points // 4], jnp.int32).reshape(1, 2, 1)
    places = lax.iota(jnp.int32, period)
    turns = (modes[..., None] * places + quarter[..., None]) % points
    basis = jnp.cos(turns.astype(jnp.float32) * (2.0 * math.pi / points)).reshape(-1, period)
    fwd = (basis * math.sqrt(2.0 / points)).astype(jnp.bfloat16)
    ratio = math.sqrt(points / (2.0 * total_modes))
    if ratio == 2.0 ** round(math.log2(ratio)):
        fwd = lax.optimization_barrier(fwd)
        inv = fwd
    else:
        inv = (basis * math.sqrt(1.0 / total_modes)).astype(jnp.bfloat16)
        ratio = 1.0

    flat = field.reshape(-1, points)
    summed = flat[:, :period].astype(jnp.float32)
    for n in range(1, points // period):
        summed = summed + flat[:, n * period : (n + 1) * period].astype(jnp.float32)
    high = summed.astype(jnp.bfloat16)
    low = (summed - high.astype(jnp.float32)).astype(jnp.bfloat16)
    rows = jnp.concatenate([high, low], axis=1)
    spec_t = lax.dot_general(
        jnp.concatenate([fwd, fwd], axis=1), rows, (((1,), (1,)), ((), ())),
        preferred_element_type=jnp.float32,
    ).astype(jnp.bfloat16)

    sent = spec_t.reshape(devices, 2 * per_dev, row_count)
    got = lax.all_to_all(sent, ("chan", "lat"), 0, 0, tiled=True)
    got = got.reshape(n_chan, n_lat, 2, per_dev, chans, fields, 2, cycles)
    sign = jnp.array([[1.0, 1.0], [1.0, -1.0]], jnp.float32)
    weight = mix_weight.astype(jnp.float32).reshape(-1, n_chan, chans)
    mix_fold = (sign[:, None, None, :, None] * jnp.transpose(weight, (0, 2, 1))[None, :, :, None, :])
    mix_fold = mix_fold.astype(jnp.bfloat16)
    folded = jnp.einsum(
        "pokhC,CLqskthr->sptqoLr", mix_fold, got, preferred_element_type=jnp.float32
    ).astype(jnp.bfloat16)
    folded = folded.reshape(per_dev, 2, fields, 2, -1, n_lat * cycles)

    leg = lax.dynamic_slice_in_dim(legendre, chan_index * per_dev, per_dev, 1)
    coefficients = jnp.einsum(
        "sptqor,psri->sptqoi", folded, leg, preferred_element_type=jnp.float32
    )
    all_gain = lax.all_gather(spectral_gain, "chan", axis=0, tiled=True)
    gain_par = jnp.transpose(all_gain.reshape(-1, half_deg, 2), (2, 0, 1))
    own_modes = lax.dynamic_slice_in_dim(
        modes.reshape(-1), (chan_index * n_lat + lat_index) * per_dev, per_dev, 0
    )
    degree = 2 * lax.iota(jnp.int32, half_deg)[None, :] + lax.iota(jnp.int32, 2)[:, None]
    allowed = degree[None, :, :] >= own_modes[:, None, None]
    filtered = jnp.where(
        allowed[:, :, None, None, None, :],
        gain_par[None, :, None, None, :, :] * coefficients,
        0.0,
    ).astype(jnp.bfloat16)
    synthesis = jnp.einsum(
        "sptqoi,psri->sptqor", filtered, leg, preferred_element_type=jnp.float32
    )
    back = jnp.stack(
        [synthesis[:, 0] + synthesis[:, 1], synthesis[:, 0] - synthesis[:, 1]], axis=1
    ).astype(jnp.bfloat16)
    back = back.reshape(per_dev, 2, fields, 2, n_chan, chans, n_lat, cycles)
    leaving = jnp.transpose(back, (4, 6, 3, 0, 5, 2, 1, 7)).reshape(devices, 2 * per_dev, row_count)
    returned = lax.all_to_all(leaving, ("chan", "lat"), 0, 0, tiled=True)
    returned = returned.reshape(2 * total_modes, row_count)

    waveform = lax.dot_general(
        returned, inv, (((0,), (0,)), ((), ())), preferred_element_type=jnp.float32
    ) * ratio
    waveform = waveform.reshape(chans, fields, -1, period)
    primal_h = waveform[:, 0]
    sigmoid_h = jax.nn.sigmoid(primal_h)
    slope_h = sigmoid_h * (1.0 + primal_h * (1.0 - sigmoid_h))
    gain_h = primal_h * sigmoid_h
    flat = field.reshape(chans, fields, -1, points)
    pieces = []
    for n in range(points // period):
        initial = flat[:, :, :, n * period : (n + 1) * period].astype(jnp.float32)
        primal = initial[:, 0] + gain_h
        tangents = initial[:, 1:] + slope_h[:, None] * waveform[:, 1:]
        pieces.append(jnp.concatenate([primal[:, None], tangents], axis=1).astype(jnp.bfloat16))
    out = jnp.concatenate(pieces, axis=3)
    return out.reshape(field.shape)


def solution(mesh):
    n_lat = mesh.shape["lat"]
    n_chan = mesh.shape["chan"]
    placed = (
        P("chan", None, None, "lat", None),
        P(),
        P("chan", None),
        P(None, "lat", None, None),
        P(),
    )

    def body(field, mix_weight, spectral_gain, legendre, slot_mode):
        return local(field, mix_weight, spectral_gain, legendre, slot_mode, n_lat, n_chan)

    return jax.shard_map(
        body,
        mesh=mesh,
        in_specs=placed,
        out_specs=P("chan", None, None, "lat", None),
        check_vma=False,
    )
```

```python
import math

import jax
import jax.numpy as jnp
from jax import lax
from jax.sharding import PartitionSpec as P


def local(field, mix_weight, spectral_gain, legendre, slot_mode, n_lat, n_chan):
    chans = field.shape[0]
    fields = field.shape[1]
    cycles = field.shape[3]
    points = field.shape[4]
    total_modes = slot_mode.shape[0]
    degrees = spectral_gain.shape[1]
    half_deg = degrees // 2
    step_size = degrees // total_modes
    period = points // math.gcd(points, step_size)
    devices = n_lat * n_chan
    per_dev = total_modes // devices
    lat_index = lax.axis_index("lat")
    chan_index = lax.axis_index("chan")
    row_count = chans * fields * 2 * cycles

    modes = (slot_mode * step_size).reshape(n_lat, n_chan, per_dev)
    modes = jnp.transpose(modes, (1, 0, 2)).reshape(devices, 1, per_dev)
    quarter = jnp.array([0, points // 4], jnp.int32).reshape(1, 2, 1)
    lanes = min(128, period)
    blocks = period // lanes
    scale = 2.0 * math.pi / points
    hi_turns = (modes[..., None] * (lax.iota(jnp.int32, blocks) * lanes) + quarter[..., None]) % points
    lo_turns = (modes[..., None] * lax.iota(jnp.int32, lanes)) % points
    hi_angle = hi_turns.astype(jnp.float32) * scale
    lo_angle = lo_turns.astype(jnp.float32) * scale
    ca, sa = jnp.cos(hi_angle)[..., None], jnp.sin(hi_angle)[..., None]
    cb, sb = jnp.cos(lo_angle)[..., None, :], jnp.sin(lo_angle)[..., None, :]
    basis = (ca * cb - sa * sb).reshape(-1, period)
    fwd = (basis * math.sqrt(2.0 / points)).astype(jnp.bfloat16)
    ratio = math.sqrt(points / (2.0 * total_modes))
    if ratio == 2.0 ** round(math.log2(ratio)):
        fwd = lax.optimization_barrier(fwd)
        inv = fwd
    else:
        inv = (basis * math.sqrt(1.0 / total_modes)).astype(jnp.bfloat16)
        ratio = 1.0

    leg = lax.dynamic_slice_in_dim(legendre, chan_index * per_dev, per_dev, 1)
    all_gain = lax.all_gather(spectral_gain, "chan", axis=0, tiled=True)
    gain_par = jnp.transpose(all_gain.reshape(-1, half_deg, 2), (2, 0, 1))
    own_modes = lax.dynamic_slice_in_dim(
        modes.reshape(-1), (chan_index * n_lat + lat_index) * per_dev, per_dev, 0
    )
    degree = 2 * lax.iota(jnp.int32, half_deg)[None, :] + lax.iota(jnp.int32, 2)[:, None]
    allowed = degree[None, :, :] >= own_modes[:, None, None]

    def chain(part):
        flat = part.reshape(-1, points)
        summed = flat[:, :period].astype(jnp.float32)
        for n in range(1, points // period):
            summed = summed + flat[:, n * period : (n + 1) * period].astype(jnp.float32)
        high = summed.astype(jnp.bfloat16)
        low = (summed - high.astype(jnp.float32)).astype(jnp.bfloat16)
        rows = jnp.concatenate([high, low], axis=1)
        spec_t = lax.dot_general(
            jnp.concatenate([fwd, fwd], axis=1), rows, (((1,), (1,)), ((), ())),
            preferred_element_type=jnp.float32,
        ).astype(jnp.bfloat16)

        row_count = rows.shape[0]
        sent = spec_t.reshape(devices, 2 * per_dev, row_count)
        got = lax.all_to_all(sent, ("chan", "lat"), 0, 0, tiled=True)
        got = got.reshape(n_chan, n_lat, 2, per_dev, chans, part.shape[1], 2, cycles)
        sign = jnp.array([[1.0, 1.0], [1.0, -1.0]], jnp.float32)
        weight = mix_weight.astype(jnp.float32).reshape(-1, n_chan, chans)
        mix_fold = (sign[:, None, None, :, None] * jnp.transpose(weight, (0, 2, 1))[None, :, :, None, :])
        mix_fold = mix_fold.astype(jnp.bfloat16)
        folded = jnp.einsum(
            "pokhC,CLqskthr->sptqoLr", mix_fold, got, preferred_element_type=jnp.float32
        ).astype(jnp.bfloat16)
        folded = folded.reshape(per_dev, 2, part.shape[1], 2, -1, n_lat * cycles)

        coefficients = jnp.einsum(
            "sptqor,psri->sptqoi", folded, leg, preferred_element_type=jnp.float32
        )
        filtered = jnp.where(
            allowed[:, :, None, None, None, :],
            gain_par[None, :, None, None, :, :] * coefficients,
            0.0,
        ).astype(jnp.bfloat16)
        synthesis = jnp.einsum(
            "sptqoi,psri->sptqor", filtered, leg, preferred_element_type=jnp.float32
        )
        back = jnp.stack(
            [synthesis[:, 0] + synthesis[:, 1], synthesis[:, 0] - synthesis[:, 1]], axis=1
        ).astype(jnp.bfloat16)
        back = back.reshape(per_dev, 2, part.shape[1], 2, n_chan, chans, n_lat, cycles)
        leaving = jnp.transpose(back, (4, 6, 3, 0, 5, 2, 1, 7)).reshape(devices, 2 * per_dev, row_count)
        returned = lax.all_to_all(leaving, ("chan", "lat"), 0, 0, tiled=True)
        returned = returned.reshape(2 * total_modes, row_count)

        waveform = lax.dot_general(
            returned, inv, (((0,), (0,)), ((), ())), preferred_element_type=jnp.float32
        ) * ratio
        return waveform.reshape(chans, part.shape[1], -1, period)

    waveform = jnp.concatenate([chain(field[:, t : t + 1]) for t in range(fields)], axis=1)
    primal_h = waveform[:, 0]
    sigmoid_h = jax.nn.sigmoid(primal_h)
    slope_h = sigmoid_h * (1.0 + primal_h * (1.0 - sigmoid_h))
    gain_h = primal_h * sigmoid_h
    flat = field.reshape(chans, fields, -1, points)
    pieces = []
    for n in range(points // period):
        initial = flat[:, :, :, n * period : (n + 1) * period].astype(jnp.float32)
        primal = initial[:, 0] + gain_h
        tangents = initial[:, 1:] + slope_h[:, None] * waveform[:, 1:]
        pieces.append(jnp.concatenate([primal[:, None], tangents], axis=1).astype(jnp.bfloat16))
    out = jnp.concatenate(pieces, axis=3)
    return out.reshape(field.shape)


def solution(mesh):
    n_lat = mesh.shape["lat"]
    n_chan = mesh.shape["chan"]
    placed = (
        P("chan", None, None, "lat", None),
        P(),
        P("chan", None),
        P(None, "lat", None, None),
        P(),
    )

    def body(field, mix_weight, spectral_gain, legendre, slot_mode):
        return local(field, mix_weight, spectral_gain, legendre, slot_mode, n_lat, n_chan)

    return jax.shard_map(
        body,
        mesh=mesh,
        in_specs=placed,
        out_specs=P("chan", None, None, "lat", None),
        check_vma=False,
    )
```

```python
import math

import jax
import jax.numpy as jnp
from jax import lax
from jax.sharding import PartitionSpec as P


def local(field, mix_weight, spectral_gain, legendre, slot_mode, n_lat, n_chan):
    chans = field.shape[0]
    fields = field.shape[1]
    cycles = field.shape[3]
    points = field.shape[4]
    total_modes = slot_mode.shape[0]
    degrees = spectral_gain.shape[1]
    half_deg = degrees // 2
    step_size = degrees // total_modes
    period = points // math.gcd(points, step_size)
    devices = n_lat * n_chan
    per_dev = total_modes // devices
    lat_index = lax.axis_index("lat")
    chan_index = lax.axis_index("chan")
    row_count = chans * fields * 2 * cycles

    modes = (slot_mode * step_size).reshape(n_lat, n_chan, per_dev)
    modes = jnp.transpose(modes, (1, 0, 2)).reshape(devices, 1, per_dev)
    quarter = jnp.array([0, points // 4], jnp.int32).reshape(1, 2, 1)
    lanes = min(128, period)
    blocks = period // lanes
    scale = 2.0 * math.pi / points
    hi_turns = (modes[..., None] * (lax.iota(jnp.int32, blocks) * lanes) + quarter[..., None]) % points
    lo_turns = (modes[..., None] * lax.iota(jnp.int32, lanes)) % points
    hi_angle = hi_turns.astype(jnp.float32) * scale
    lo_angle = lo_turns.astype(jnp.float32) * scale
    ca, sa = jnp.cos(hi_angle)[..., None], jnp.sin(hi_angle)[..., None]
    cb, sb = jnp.cos(lo_angle)[..., None, :], jnp.sin(lo_angle)[..., None, :]
    basis = (ca * cb - sa * sb).reshape(-1, period)
    fwd = (basis * math.sqrt(2.0 / points)).astype(jnp.bfloat16)
    ratio = math.sqrt(points / (2.0 * total_modes))
    if ratio == 2.0 ** round(math.log2(ratio)):
        fwd = lax.optimization_barrier(fwd)
        inv = fwd
    else:
        inv = (basis * math.sqrt(1.0 / total_modes)).astype(jnp.bfloat16)
        ratio = 1.0

    flat = field.reshape(-1, points)
    summed = flat[:, :period].astype(jnp.float32)
    for n in range(1, points // period):
        summed = summed + flat[:, n * period : (n + 1) * period].astype(jnp.float32)
    high = summed.astype(jnp.bfloat16)
    low = (summed - high.astype(jnp.float32)).astype(jnp.bfloat16)
    rows = jnp.concatenate([high, low], axis=1)
    spec_t = lax.dot_general(
        jnp.concatenate([fwd, fwd], axis=1), rows, (((1,), (1,)), ((), ())),
        preferred_element_type=jnp.float32,
    ).astype(jnp.bfloat16)

    sent = spec_t.reshape(devices, 2 * per_dev, row_count)
    got = lax.all_to_all(sent, ("chan", "lat"), 0, 0, tiled=True)
    got = got.reshape(n_chan, n_lat, 2, per_dev, chans, fields, 2, cycles)
    sign = jnp.array([[1.0, 1.0], [1.0, -1.0]], jnp.float32)
    weight = mix_weight.astype(jnp.float32).reshape(-1, n_chan, chans)
    mix_fold = (sign[:, None, None, :, None] * jnp.transpose(weight, (0, 2, 1))[None, :, :, None, :])
    mix_fold = mix_fold.astype(jnp.bfloat16)
    folded = jnp.einsum(
        "pokhC,CLqskthr->sptqoLr", mix_fold, got, preferred_element_type=jnp.float32
    ).astype(jnp.bfloat16)
    folded = folded.reshape(per_dev, 2, fields, 2, -1, n_lat * cycles)

    leg = lax.dynamic_slice_in_dim(legendre, chan_index * per_dev, per_dev, 1)
    coefficients = jnp.einsum(
        "sptqor,psri->sptqoi", folded, leg, preferred_element_type=jnp.float32
    )
    all_gain = lax.all_gather(spectral_gain, "chan", axis=0, tiled=True)
    gain_par = jnp.transpose(all_gain.reshape(-1, half_deg, 2), (2, 0, 1))
    own_modes = lax.dynamic_slice_in_dim(
        modes.reshape(-1), (chan_index * n_lat + lat_index) * per_dev, per_dev, 0
    )
    degree = 2 * lax.iota(jnp.int32, half_deg)[None, :] + lax.iota(jnp.int32, 2)[:, None]
    allowed = degree[None, :, :] >= own_modes[:, None, None]
    sign = jnp.array([[1.0, 1.0], [1.0, -1.0]], jnp.float32).reshape(1, 2, 2, 1, 1, 1, 1)
    scaled = gain_par[None, :, None, None, :, :] * coefficients
    filtered = jnp.where(
        allowed[:, None, :, None, None, None, :], sign * scaled[:, None], 0.0
    ).astype(jnp.bfloat16)
    back = jnp.einsum(
        "shptqoi,psri->shtqor", filtered, leg, preferred_element_type=jnp.float32
    ).astype(jnp.bfloat16)
    back = back.reshape(per_dev, 2, fields, 2, n_chan, chans, n_lat, cycles)
    leaving = jnp.transpose(back, (4, 6, 3, 0, 5, 2, 1, 7)).reshape(devices, 2 * per_dev, row_count)
    returned = lax.all_to_all(leaving, ("chan", "lat"), 0, 0, tiled=True)
    returned = returned.reshape(2 * total_modes, row_count)

    waveform = lax.dot_general(
        returned, inv, (((0,), (0,)), ((), ())), preferred_element_type=jnp.float32
    ) * ratio
    waveform = waveform.reshape(chans, fields, -1, period)
    primal_h = waveform[:, 0]
    sigmoid_h = jax.nn.sigmoid(primal_h)
    slope_h = sigmoid_h * (1.0 + primal_h * (1.0 - sigmoid_h))
    gain_h = primal_h * sigmoid_h
    flat = field.reshape(chans, fields, -1, points)
    pieces = []
    for n in range(points // period):
        initial = flat[:, :, :, n * period : (n + 1) * period].astype(jnp.float32)
        primal = initial[:, 0] + gain_h
        tangents = initial[:, 1:] + slope_h[:, None] * waveform[:, 1:]
        pieces.append(jnp.concatenate([primal[:, None], tangents], axis=1).astype(jnp.bfloat16))
    out = jnp.concatenate(pieces, axis=3)
    return out.reshape(field.shape)


def solution(mesh):
    n_lat = mesh.shape["lat"]
    n_chan = mesh.shape["chan"]
    placed = (
        P("chan", None, None, "lat", None),
        P(),
        P("chan", None),
        P(None, "lat", None, None),
        P(),
    )

    def body(field, mix_weight, spectral_gain, legendre, slot_mode):
        return local(field, mix_weight, spectral_gain, legendre, slot_mode, n_lat, n_chan)

    return jax.shard_map(
        body,
        mesh=mesh,
        in_specs=placed,
        out_specs=P("chan", None, None, "lat", None),
        check_vma=False,
    )
```

```python
import functools
import math

import jax
import jax.numpy as jnp
from jax import lax
from jax.experimental import pallas as pl
from jax.experimental.pallas import tpu as pltpu
from jax.sharding import PartitionSpec as P


def legendre_kernel(modes_ref, base_ref, folded_ref, leg_ref, gain_ref, out_ref, *, block):
    s = pl.program_id(0)
    mode = modes_ref[s]
    half_deg = leg_ref.shape[-1]
    rows = folded_ref.shape[-2]
    north = folded_ref.shape[-1]
    syn = []
    for p in range(2):
        lhs = folded_ref[0, p]
        acc = jnp.zeros((rows, north), jnp.float32)
        for b in range(half_deg // block):
            def step(acc, p=p, b=b):
                table = leg_ref[p, 0, :, b * block : (b + 1) * block]
                coef = jnp.dot(lhs, table, preferred_element_type=jnp.float32)
                degree = 2 * (b * block + lax.broadcasted_iota(jnp.int32, (1, block), 1)) + p
                kept = jnp.where(
                    degree >= mode, gain_ref[p, :, b * block : (b + 1) * block] * coef, 0.0
                ).astype(jnp.bfloat16)
                return acc + lax.dot_general(
                    kept, table, (((1,), (1,)), ((), ())), preferred_element_type=jnp.float32
                )
            top = 2 * ((b + 1) * block - 1) + p
            acc = lax.cond(top >= mode, step, lambda a: a, acc)
        syn.append(acc)
    out_ref[0, 0] = (syn[0] + syn[1]).astype(out_ref.dtype)
    out_ref[0, 1] = (syn[0] - syn[1]).astype(out_ref.dtype)


def legendre_stage(folded, legendre, gain_rows, own_modes, base, block=256):
    per_dev, _, rows, north = folded.shape
    half_deg = legendre.shape[-1]
    grid_spec = pltpu.PrefetchScalarGridSpec(
        num_scalar_prefetch=2,
        grid=(per_dev,),
        in_specs=[
            pl.BlockSpec((1, 2, rows, north), lambda s, m, b: (s, 0, 0, 0)),
            pl.BlockSpec((2, 1, north, half_deg), lambda s, m, b: (0, b[0] + s, 0, 0)),
            pl.BlockSpec((2, rows, half_deg), lambda s, m, b: (0, 0, 0)),
        ],
        out_specs=pl.BlockSpec((1, 2, rows, north), lambda s, m, b: (s, 0, 0, 0)),
    )
    flops = 8 * per_dev * rows * north * half_deg
    return pl.pallas_call(
        functools.partial(legendre_kernel, block=block),
        grid_spec=grid_spec,
        out_shape=jax.ShapeDtypeStruct((per_dev, 2, rows, north), jnp.bfloat16),
        compiler_params=pltpu.CompilerParams(vmem_limit_bytes=48 * 1024 * 1024),
        cost_estimate=pl.CostEstimate(
            flops=flops, transcendentals=0,
            bytes_accessed=2 * per_dev * north * half_deg * 2 + 4 * folded.size + 4 * gain_rows.size,
        ),
    )(own_modes, base, folded, legendre, gain_rows)


def local(field, mix_weight, spectral_gain, legendre, slot_mode, n_lat, n_chan):
    chans = field.shape[0]
    fields = field.shape[1]
    cycles = field.shape[3]
    points = field.shape[4]
    total_modes = slot_mode.shape[0]
    degrees = spectral_gain.shape[1]
    half_deg = degrees // 2
    step_size = degrees // total_modes
    period = points // math.gcd(points, step_size)
    devices = n_lat * n_chan
    per_dev = total_modes // devices
    lat_index = lax.axis_index("lat")
    chan_index = lax.axis_index("chan")
    row_count = chans * fields * 2 * cycles

    modes = (slot_mode * step_size).reshape(n_lat, n_chan, per_dev)
    modes = jnp.transpose(modes, (1, 0, 2)).reshape(devices, 1, per_dev)
    quarter = jnp.array([0, points // 4], jnp.int32).reshape(1, 2, 1)
    lanes = min(128, period)
    blocks = period // lanes
    scale = 2.0 * math.pi / points
    hi_turns = (modes[..., None] * (lax.iota(jnp.int32, blocks) * lanes) + quarter[..., None]) % points
    lo_turns = (modes[..., None] * lax.iota(jnp.int32, lanes)) % points
    hi_angle = hi_turns.astype(jnp.float32) * scale
    lo_angle = lo_turns.astype(jnp.float32) * scale
    ca, sa = jnp.cos(hi_angle)[..., None], jnp.sin(hi_angle)[..., None]
    cb, sb = jnp.cos(lo_angle)[..., None, :], jnp.sin(lo_angle)[..., None, :]
    basis = (ca * cb - sa * sb).reshape(-1, period)
    fwd = (basis * math.sqrt(2.0 / points)).astype(jnp.bfloat16)
    ratio = math.sqrt(points / (2.0 * total_modes))
    if ratio == 2.0 ** round(math.log2(ratio)):
        fwd = lax.optimization_barrier(fwd)
        inv = fwd
    else:
        inv = (basis * math.sqrt(1.0 / total_modes)).astype(jnp.bfloat16)
        ratio = 1.0

    flat = field.reshape(-1, points)
    summed = flat[:, :period].astype(jnp.float32)
    for n in range(1, points // period):
        summed = summed + flat[:, n * period : (n + 1) * period].astype(jnp.float32)
    high = summed.astype(jnp.bfloat16)
    low = (summed - high.astype(jnp.float32)).astype(jnp.bfloat16)
    rows = jnp.concatenate([high, low], axis=1)
    spec_t = lax.dot_general(
        jnp.concatenate([fwd, fwd], axis=1), rows, (((1,), (1,)), ((), ())),
        preferred_element_type=jnp.float32,
    ).astype(jnp.bfloat16)

    sent = spec_t.reshape(devices, 2 * per_dev, row_count)
    got = lax.all_to_all(sent, ("chan", "lat"), 0, 0, tiled=True)
    got = got.reshape(n_chan, n_lat, 2, per_dev, chans, fields, 2, cycles)
    sign = jnp.array([[1.0, 1.0], [1.0, -1.0]], jnp.float32)
    weight = mix_weight.astype(jnp.float32).reshape(-1, n_chan, chans)
    mix_fold = (sign[:, None, None, :, None] * jnp.transpose(weight, (0, 2, 1))[None, :, :, None, :])
    mix_fold = mix_fold.astype(jnp.bfloat16)
    folded = jnp.einsum(
        "pokhC,CLqskthr->sptqoLr", mix_fold, got, preferred_element_type=jnp.float32
    ).astype(jnp.bfloat16)
    folded = folded.reshape(per_dev, 2, fields, 2, -1, n_lat * cycles)

    all_gain = lax.all_gather(spectral_gain, "chan", axis=0, tiled=True)
    gain_par = jnp.transpose(all_gain.reshape(-1, half_deg, 2), (2, 0, 1))
    own_modes = lax.dynamic_slice_in_dim(
        modes.reshape(-1), (chan_index * n_lat + lat_index) * per_dev, per_dev, 0
    )
    rows_x = folded.shape[2] * folded.shape[3] * folded.shape[4]
    gain_rows = jnp.tile(gain_par, (1, rows_x // gain_par.shape[1], 1))
    base = (chan_index * per_dev).astype(jnp.int32).reshape(1)
    back = legendre_stage(
        folded.reshape(per_dev, 2, rows_x, -1), legendre, gain_rows, own_modes, base
    )
    back = back.reshape(per_dev, 2, fields, 2, n_chan, chans, n_lat, cycles)
    leaving = jnp.transpose(back, (4, 6, 3, 0, 5, 2, 1, 7)).reshape(devices, 2 * per_dev, row_count)
    returned = lax.all_to_all(leaving, ("chan", "lat"), 0, 0, tiled=True)
    returned = returned.reshape(2 * total_modes, row_count)

    waveform = lax.dot_general(
        returned, inv, (((0,), (0,)), ((), ())), preferred_element_type=jnp.float32
    ) * ratio
    waveform = waveform.reshape(chans, fields, -1, period)
    primal_h = waveform[:, 0]
    sigmoid_h = jax.nn.sigmoid(primal_h)
    slope_h = sigmoid_h * (1.0 + primal_h * (1.0 - sigmoid_h))
    gain_h = primal_h * sigmoid_h
    flat = field.reshape(chans, fields, -1, points)
    pieces = []
    for n in range(points // period):
        initial = flat[:, :, :, n * period : (n + 1) * period].astype(jnp.float32)
        primal = initial[:, 0] + gain_h
        tangents = initial[:, 1:] + slope_h[:, None] * waveform[:, 1:]
        pieces.append(jnp.concatenate([primal[:, None], tangents], axis=1).astype(jnp.bfloat16))
    out = jnp.concatenate(pieces, axis=3)
    return out.reshape(field.shape)


def solution(mesh):
    n_lat = mesh.shape["lat"]
    n_chan = mesh.shape["chan"]
    placed = (
        P("chan", None, None, "lat", None),
        P(),
        P("chan", None),
        P(None, "lat", None, None),
        P(),
    )

    def body(field, mix_weight, spectral_gain, legendre, slot_mode):
        return local(field, mix_weight, spectral_gain, legendre, slot_mode, n_lat, n_chan)

    return jax.shard_map(
        body,
        mesh=mesh,
        in_specs=placed,
        out_specs=P("chan", None, None, "lat", None),
        check_vma=False,
    )
```

```python
import functools
import math

import jax
import jax.numpy as jnp
from jax import lax
from jax.experimental import pallas as pl
from jax.experimental.pallas import tpu as pltpu
from jax.sharding import PartitionSpec as P


def block_swap(x, piece):
    rows, width = x.shape
    group = 128 // piece
    row = lax.broadcasted_iota(jnp.int32, x.shape, 0) % group
    blk = (lax.broadcasted_iota(jnp.int32, x.shape, 1) % 128) // piece
    out = jnp.zeros_like(x)
    for d in range(1 - group, group):
        moved = x if d == 0 else pltpu.roll(x, (-piece * d) % width, 1)
        keep = (blk == row) & (row + d >= 0) & (row + d < group)
        moved = jnp.where(keep, moved, 0.0)
        out = out + (moved if d == 0 else pltpu.roll(moved, d % rows, 0))
    return out


def gather_kernel(got_ref, mix_ref, out_ref, stage_ref, *, piece, per_dev, pairs):
    n_chan = got_ref.shape[0]
    lat_rows = got_ref.shape[2]
    group = 128 // piece

    def one(qs, carry):
        for c in range(n_chan):
            swapped = block_swap(got_ref[c, qs].astype(jnp.float32), piece)
            for th in range(pairs):
                for tile in range(lat_rows // group):
                    stage_ref[qs, th // 2, c, th % 2, :, tile * 128 : (tile + 1) * 128] = swapped[
                        tile * group : (tile + 1) * group, th * 128 : (th + 1) * 128
                    ]
        q = qs // per_dev
        s = qs % per_dev
        for t in range(pairs // 2):
            block = stage_ref[qs, t]
            block = block.reshape(-1, block.shape[-1]).astype(jnp.bfloat16)
            mixed = jnp.dot(mix_ref[...], block, preferred_element_type=jnp.float32)
            half = mixed.shape[0] // 2
            for p in range(2):
                out_ref[s, p, t, q] = mixed[p * half : (p + 1) * half].astype(out_ref.dtype)
        return carry

    lax.fori_loop(0, got_ref.shape[1], one, 0)


def scatter_kernel(back_ref, out_ref, *, piece, per_dev, fields):
    n_chan = out_ref.shape[0]
    lat_rows = out_ref.shape[2]
    group = 128 // piece
    chans = back_ref.shape[2] // (fields * 2)

    def one(qs, carry):
        q = qs // per_dev
        s = qs % per_dev
        for t in range(fields):
            for h in range(2):
                start = (t * 2 + q) * chans
                part = back_ref[s, h, pl.ds(pl.multiple_of(start, 8), chans)].astype(jnp.float32)
                swapped = block_swap(part, piece)
                th = t * 2 + h
                for c in range(n_chan):
                    column = jnp.concatenate(
                        [
                            swapped[c * group : (c + 1) * group, tile * 128 : (tile + 1) * 128]
                            for tile in range(lat_rows // group)
                        ],
                        axis=0,
                    )
                    out_ref[c, qs, :, th * 128 : (th + 1) * 128] = column.astype(out_ref.dtype)
        return carry

    lax.fori_loop(0, out_ref.shape[1], one, 0)


def legendre_kernel(modes_ref, base_ref, folded_ref, leg_ref, gain_ref, out_ref, *, block):
    s = pl.program_id(0)
    mode = modes_ref[s]
    half_deg = leg_ref.shape[-1]
    rows = folded_ref.shape[-2]
    north = folded_ref.shape[-1]
    syn = []
    for p in range(2):
        lhs = folded_ref[0, p]
        acc = jnp.zeros((rows, north), jnp.float32)
        for b in range(half_deg // block):
            def step(acc, p=p, b=b):
                table = leg_ref[p, 0, :, b * block : (b + 1) * block]
                coef = jnp.dot(lhs, table, preferred_element_type=jnp.float32)
                degree = 2 * (b * block + lax.broadcasted_iota(jnp.int32, (1, block), 1)) + p
                kept = jnp.where(
                    degree >= mode, gain_ref[p, :, b * block : (b + 1) * block] * coef, 0.0
                ).astype(jnp.bfloat16)
                return acc + lax.dot_general(
                    kept, table, (((1,), (1,)), ((), ())), preferred_element_type=jnp.float32
                )
            top = 2 * ((b + 1) * block - 1) + p
            acc = lax.cond(top >= mode, step, lambda a: a, acc)
        syn.append(acc)
    out_ref[0, 0] = (syn[0] + syn[1]).astype(out_ref.dtype)
    out_ref[0, 1] = (syn[0] - syn[1]).astype(out_ref.dtype)


def legendre_stage(folded, legendre, gain_rows, own_modes, base, block=256):
    per_dev, _, rows, north = folded.shape
    half_deg = legendre.shape[-1]
    grid_spec = pltpu.PrefetchScalarGridSpec(
        num_scalar_prefetch=2,
        grid=(per_dev,),
        in_specs=[
            pl.BlockSpec((1, 2, rows, north), lambda s, m, b: (s, 0, 0, 0)),
            pl.BlockSpec((2, 1, north, half_deg), lambda s, m, b: (0, b[0] + s, 0, 0)),
            pl.BlockSpec((2, rows, half_deg), lambda s, m, b: (0, 0, 0)),
        ],
        out_specs=pl.BlockSpec((1, 2, rows, north), lambda s, m, b: (s, 0, 0, 0)),
    )
    flops = 8 * per_dev * rows * north * half_deg
    return pl.pallas_call(
        functools.partial(legendre_kernel, block=block),
        grid_spec=grid_spec,
        out_shape=jax.ShapeDtypeStruct((per_dev, 2, rows, north), jnp.bfloat16),
        compiler_params=pltpu.CompilerParams(vmem_limit_bytes=48 * 1024 * 1024),
        cost_estimate=pl.CostEstimate(
            flops=flops, transcendentals=0,
            bytes_accessed=2 * per_dev * north * half_deg * 2 + 4 * folded.size + 4 * gain_rows.size,
        ),
    )(own_modes, base, folded, legendre, gain_rows)


def local(field, mix_weight, spectral_gain, legendre, slot_mode, n_lat, n_chan):
    chans = field.shape[0]
    fields = field.shape[1]
    cycles = field.shape[3]
    points = field.shape[4]
    total_modes = slot_mode.shape[0]
    degrees = spectral_gain.shape[1]
    half_deg = degrees // 2
    step_size = degrees // total_modes
    period = points // math.gcd(points, step_size)
    devices = n_lat * n_chan
    per_dev = total_modes // devices
    lat_index = lax.axis_index("lat")
    chan_index = lax.axis_index("chan")
    row_count = chans * fields * 2 * cycles

    modes = (slot_mode * step_size).reshape(n_lat, n_chan, per_dev)
    modes = jnp.transpose(modes, (1, 0, 2)).reshape(devices, 1, per_dev)
    quarter = jnp.array([0, points // 4], jnp.int32).reshape(1, 2, 1)
    lanes = min(128, period)
    blocks = period // lanes
    scale = 2.0 * math.pi / points
    hi_turns = (modes[..., None] * (lax.iota(jnp.int32, blocks) * lanes) + quarter[..., None]) % points
    lo_turns = (modes[..., None] * lax.iota(jnp.int32, lanes)) % points
    hi_angle = hi_turns.astype(jnp.float32) * scale
    lo_angle = lo_turns.astype(jnp.float32) * scale
    ca, sa = jnp.cos(hi_angle)[..., None], jnp.sin(hi_angle)[..., None]
    cb, sb = jnp.cos(lo_angle)[..., None, :], jnp.sin(lo_angle)[..., None, :]
    basis = (ca * cb - sa * sb).reshape(-1, period)
    fwd = (basis * math.sqrt(2.0 / points)).astype(jnp.bfloat16)
    ratio = math.sqrt(points / (2.0 * total_modes))
    if ratio == 2.0 ** round(math.log2(ratio)):
        fwd = lax.optimization_barrier(fwd)
        inv = fwd
    else:
        inv = (basis * math.sqrt(1.0 / total_modes)).astype(jnp.bfloat16)
        ratio = 1.0

    flat = jnp.transpose(field, (1, 2, 0, 3, 4)).reshape(-1, points)
    summed = flat[:, :period].astype(jnp.float32)
    for n in range(1, points // period):
        summed = summed + flat[:, n * period : (n + 1) * period].astype(jnp.float32)
    high = summed.astype(jnp.bfloat16)
    low = (summed - high.astype(jnp.float32)).astype(jnp.bfloat16)
    rows = jnp.concatenate([high, low], axis=1)
    spec_t = lax.dot_general(
        jnp.concatenate([fwd, fwd], axis=1), rows, (((1,), (1,)), ((), ())),
        preferred_element_type=jnp.float32,
    ).astype(jnp.bfloat16)

    sent = spec_t.reshape(devices, 2 * per_dev, row_count)
    got = lax.all_to_all(sent, ("chan", "lat"), 0, 0, tiled=True)
    got = jnp.transpose(got.reshape(n_chan, n_lat, 2 * per_dev, row_count), (0, 2, 1, 3))
    sign = jnp.array([[1.0, 1.0], [1.0, -1.0]], jnp.float32)
    weight = mix_weight.astype(jnp.float32).reshape(-1, n_chan, chans)
    mix_fold = sign[:, None, None, :, None] * weight[None, :, :, None, :]
    mix_fold = mix_fold.reshape(2 * weight.shape[0], -1).astype(jnp.bfloat16)
    piece = cycles
    folded = pl.pallas_call(
        functools.partial(gather_kernel, piece=piece, per_dev=per_dev, pairs=2 * fields),
        out_shape=jax.ShapeDtypeStruct(
            (per_dev, 2, fields, 2, weight.shape[0], n_lat * cycles), jnp.bfloat16
        ),
        scratch_shapes=[pltpu.VMEM((2 * per_dev, fields, n_chan, 2, chans, n_lat * cycles), jnp.float32)],
        compiler_params=pltpu.CompilerParams(vmem_limit_bytes=48 * 1024 * 1024),
    )(got, mix_fold)

    all_gain = lax.all_gather(spectral_gain, "chan", axis=0, tiled=True)
    gain_par = jnp.transpose(all_gain.reshape(-1, half_deg, 2), (2, 0, 1))
    own_modes = lax.dynamic_slice_in_dim(
        modes.reshape(-1), (chan_index * n_lat + lat_index) * per_dev, per_dev, 0
    )
    rows_x = folded.shape[2] * folded.shape[3] * folded.shape[4]
    gain_rows = jnp.tile(gain_par, (1, rows_x // gain_par.shape[1], 1))
    base = (chan_index * per_dev).astype(jnp.int32).reshape(1)
    back = legendre_stage(
        folded.reshape(per_dev, 2, rows_x, -1), legendre, gain_rows, own_modes, base
    )
    spread = pl.pallas_call(
        functools.partial(scatter_kernel, piece=piece, per_dev=per_dev, fields=fields),
        out_shape=jax.ShapeDtypeStruct((n_chan, 2 * per_dev, n_lat, row_count), jnp.bfloat16),
        compiler_params=pltpu.CompilerParams(vmem_limit_bytes=48 * 1024 * 1024),
    )(back)
    leaving = jnp.transpose(spread, (0, 2, 1, 3)).reshape(devices, 2 * per_dev, row_count)
    returned = lax.all_to_all(leaving, ("chan", "lat"), 0, 0, tiled=True)
    returned = returned.reshape(2 * total_modes, row_count)

    waveform = lax.dot_general(
        returned, inv, (((0,), (0,)), ((), ())), preferred_element_type=jnp.float32
    ) * ratio
    waveform = jnp.transpose(waveform.reshape(fields, 2, chans, cycles, period), (2, 0, 1, 3, 4))
    waveform = waveform.reshape(chans, fields, -1, period)
    primal_h = waveform[:, 0]
    sigmoid_h = jax.nn.sigmoid(primal_h)
    slope_h = sigmoid_h * (1.0 + primal_h * (1.0 - sigmoid_h))
    gain_h = primal_h * sigmoid_h
    flat = field.reshape(chans, fields, -1, points)
    pieces = []
    for n in range(points // period):
        initial = flat[:, :, :, n * period : (n + 1) * period].astype(jnp.float32)
        primal = initial[:, 0] + gain_h
        tangents = initial[:, 1:] + slope_h[:, None] * waveform[:, 1:]
        pieces.append(jnp.concatenate([primal[:, None], tangents], axis=1).astype(jnp.bfloat16))
    out = jnp.concatenate(pieces, axis=3)
    return out.reshape(field.shape)


def solution(mesh):
    n_lat = mesh.shape["lat"]
    n_chan = mesh.shape["chan"]
    placed = (
        P("chan", None, None, "lat", None),
        P(),
        P("chan", None),
        P(None, "lat", None, None),
        P(),
    )

    def body(field, mix_weight, spectral_gain, legendre, slot_mode):
        return local(field, mix_weight, spectral_gain, legendre, slot_mode, n_lat, n_chan)

    return jax.shard_map(
        body,
        mesh=mesh,
        in_specs=placed,
        out_specs=P("chan", None, None, "lat", None),
        check_vma=False,
    )
```

```python
import functools
import math

import jax
import jax.numpy as jnp
from jax import lax
from jax.experimental import pallas as pl
from jax.experimental.pallas import tpu as pltpu
from jax.sharding import PartitionSpec as P


def block_swap(x, piece):
    group, width = x.shape[1], x.shape[2]
    row = lax.broadcasted_iota(jnp.int32, x.shape, 1)
    blk = lax.broadcasted_iota(jnp.int32, x.shape, 2) // piece
    out = jnp.where(blk == row, x, 0.0)
    for d in range(1, group):
        moved = pltpu.roll(x, (-piece * d) % width, 2)
        moved = jnp.where(blk == row, moved, 0.0)
        out = out + pltpu.roll(moved, d, 1)
    return out


def tiles_of(x, group):
    return jnp.stack(
        [
            x[i * group : (i + 1) * group, j * 128 : (j + 1) * 128]
            for i in range(x.shape[0] // group)
            for j in range(x.shape[1] // 128)
        ]
    )


def gather_kernel(got_ref, mix_ref, out_ref, stage_ref, *, piece, per_dev, pairs):
    n_chan = got_ref.shape[0]
    lat_rows = got_ref.shape[2]
    group = 128 // piece

    def one(qs, carry):
        for c in range(n_chan):
            swapped = block_swap(tiles_of(got_ref[c, qs].astype(jnp.float32), group), piece)
            for tile in range(lat_rows // group):
                for th in range(pairs):
                    stage_ref[qs, th // 2, c, th % 2, :, tile * 128 : (tile + 1) * 128] = swapped[
                        tile * pairs + th
                    ]
        q = qs // per_dev
        s = qs % per_dev
        for t in range(pairs // 2):
            block = stage_ref[qs, t]
            block = block.reshape(-1, block.shape[-1]).astype(jnp.bfloat16)
            mixed = jnp.dot(mix_ref[...], block, preferred_element_type=jnp.float32)
            half = mixed.shape[0] // 2
            for p in range(2):
                out_ref[s, p, t, q] = mixed[p * half : (p + 1) * half].astype(out_ref.dtype)
        return carry

    lax.fori_loop(0, got_ref.shape[1], one, 0)


def scatter_kernel(back_ref, out_ref, *, piece, per_dev, fields):
    n_chan = out_ref.shape[0]
    lat_rows = out_ref.shape[2]
    group = 128 // piece
    chans = back_ref.shape[2] // (fields * 2)

    def one(qs, carry):
        q = qs // per_dev
        s = qs % per_dev
        for t in range(fields):
            for h in range(2):
                start = (t * 2 + q) * chans
                part = back_ref[s, h, pl.ds(pl.multiple_of(start, 8), chans)].astype(jnp.float32)
                swapped = block_swap(tiles_of(part, group), piece)
                th = t * 2 + h
                lane_tiles = part.shape[1] // 128
                for c in range(n_chan):
                    column = jnp.concatenate(
                        [swapped[c * lane_tiles + tile] for tile in range(lat_rows // group)], axis=0
                    )
                    out_ref[c, qs, :, th * 128 : (th + 1) * 128] = column.astype(out_ref.dtype)
        return carry

    lax.fori_loop(0, out_ref.shape[1], one, 0)


def legendre_kernel(modes_ref, base_ref, folded_ref, leg_ref, gain_ref, out_ref, *, block):
    s = pl.program_id(0)
    mode = modes_ref[s]
    half_deg = leg_ref.shape[-1]
    rows = folded_ref.shape[-2]
    north = folded_ref.shape[-1]
    syn = []
    for p in range(2):
        lhs = folded_ref[0, p]
        acc = jnp.zeros((rows, north), jnp.float32)
        for b in range(half_deg // block):
            def step(acc, p=p, b=b):
                table = leg_ref[p, 0, :, b * block : (b + 1) * block]
                coef = jnp.dot(lhs, table, preferred_element_type=jnp.float32)
                degree = 2 * (b * block + lax.broadcasted_iota(jnp.int32, (1, block), 1)) + p
                kept = jnp.where(
                    degree >= mode, gain_ref[p, :, b * block : (b + 1) * block] * coef, 0.0
                ).astype(jnp.bfloat16)
                return acc + lax.dot_general(
                    kept, table, (((1,), (1,)), ((), ())), preferred_element_type=jnp.float32
                )
            top = 2 * ((b + 1) * block - 1) + p
            acc = lax.cond(top >= mode, step, lambda a: a, acc)
        syn.append(acc)
    out_ref[0, 0] = (syn[0] + syn[1]).astype(out_ref.dtype)
    out_ref[0, 1] = (syn[0] - syn[1]).astype(out_ref.dtype)


def legendre_stage(folded, legendre, gain_rows, own_modes, base, block=256):
    per_dev, _, rows, north = folded.shape
    half_deg = legendre.shape[-1]
    grid_spec = pltpu.PrefetchScalarGridSpec(
        num_scalar_prefetch=2,
        grid=(per_dev,),
        in_specs=[
            pl.BlockSpec((1, 2, rows, north), lambda s, m, b: (s, 0, 0, 0)),
            pl.BlockSpec((2, 1, north, half_deg), lambda s, m, b: (0, b[0] + s, 0, 0)),
            pl.BlockSpec((2, rows, half_deg), lambda s, m, b: (0, 0, 0)),
        ],
        out_specs=pl.BlockSpec((1, 2, rows, north), lambda s, m, b: (s, 0, 0, 0)),
    )
    flops = 8 * per_dev * rows * north * half_deg
    return pl.pallas_call(
        functools.partial(legendre_kernel, block=block),
        grid_spec=grid_spec,
        out_shape=jax.ShapeDtypeStruct((per_dev, 2, rows, north), jnp.bfloat16),
        compiler_params=pltpu.CompilerParams(vmem_limit_bytes=48 * 1024 * 1024),
        cost_estimate=pl.CostEstimate(
            flops=flops, transcendentals=0,
            bytes_accessed=2 * per_dev * north * half_deg * 2 + 4 * folded.size + 4 * gain_rows.size,
        ),
    )(own_modes, base, folded, legendre, gain_rows)


def local(field, mix_weight, spectral_gain, legendre, slot_mode, n_lat, n_chan):
    chans = field.shape[0]
    fields = field.shape[1]
    cycles = field.shape[3]
    points = field.shape[4]
    total_modes = slot_mode.shape[0]
    degrees = spectral_gain.shape[1]
    half_deg = degrees // 2
    step_size = degrees // total_modes
    period = points // math.gcd(points, step_size)
    devices = n_lat * n_chan
    per_dev = total_modes // devices
    lat_index = lax.axis_index("lat")
    chan_index = lax.axis_index("chan")
    row_count = chans * fields * 2 * cycles

    modes = (slot_mode * step_size).reshape(n_lat, n_chan, per_dev)
    modes = jnp.transpose(modes, (1, 0, 2)).reshape(devices, 1, per_dev)
    quarter = jnp.array([0, points // 4], jnp.int32).reshape(1, 2, 1)
    lanes = min(128, period)
    blocks = period // lanes
    scale = 2.0 * math.pi / points
    hi_turns = (modes[..., None] * (lax.iota(jnp.int32, blocks) * lanes) + quarter[..., None]) % points
    lo_turns = (modes[..., None] * lax.iota(jnp.int32, lanes)) % points
    hi_angle = hi_turns.astype(jnp.float32) * scale
    lo_angle = lo_turns.astype(jnp.float32) * scale
    ca, sa = jnp.cos(hi_angle)[..., None], jnp.sin(hi_angle)[..., None]
    cb, sb = jnp.cos(lo_angle)[..., None, :], jnp.sin(lo_angle)[..., None, :]
    basis = (ca * cb - sa * sb).reshape(-1, period)
    fwd = (basis * math.sqrt(2.0 / points)).astype(jnp.bfloat16)
    ratio = math.sqrt(points / (2.0 * total_modes))
    if ratio == 2.0 ** round(math.log2(ratio)):
        fwd = lax.optimization_barrier(fwd)
        inv = fwd
    else:
        inv = (basis * math.sqrt(1.0 / total_modes)).astype(jnp.bfloat16)
        ratio = 1.0

    flat = jnp.transpose(field, (1, 2, 0, 3, 4)).reshape(-1, points)
    summed = flat[:, :period].astype(jnp.float32)
    for n in range(1, points // period):
        summed = summed + flat[:, n * period : (n + 1) * period].astype(jnp.float32)
    high = summed.astype(jnp.bfloat16)
    low = (summed - high.astype(jnp.float32)).astype(jnp.bfloat16)
    rows = jnp.concatenate([high, low], axis=1)
    spec_t = lax.dot_general(
        jnp.concatenate([fwd, fwd], axis=1), rows, (((1,), (1,)), ((), ())),
        preferred_element_type=jnp.float32,
    ).astype(jnp.bfloat16)

    sent = spec_t.reshape(devices, 2 * per_dev, row_count)
    got = lax.all_to_all(sent, ("chan", "lat"), 0, 0, tiled=True)
    got = jnp.transpose(got.reshape(n_chan, n_lat, 2 * per_dev, row_count), (0, 2, 1, 3))
    sign = jnp.array([[1.0, 1.0], [1.0, -1.0]], jnp.float32)
    weight = mix_weight.astype(jnp.float32).reshape(-1, n_chan, chans)
    mix_fold = sign[:, None, None, :, None] * weight[None, :, :, None, :]
    mix_fold = mix_fold.reshape(2 * weight.shape[0], -1).astype(jnp.bfloat16)
    piece = cycles
    folded = pl.pallas_call(
        functools.partial(gather_kernel, piece=piece, per_dev=per_dev, pairs=2 * fields),
        out_shape=jax.ShapeDtypeStruct(
            (per_dev, 2, fields, 2, weight.shape[0], n_lat * cycles), jnp.bfloat16
        ),
        scratch_shapes=[pltpu.VMEM((2 * per_dev, fields, n_chan, 2, chans, n_lat * cycles), jnp.float32)],
        compiler_params=pltpu.CompilerParams(vmem_limit_bytes=48 * 1024 * 1024),
    )(got, mix_fold)

    all_gain = lax.all_gather(spectral_gain, "chan", axis=0, tiled=True)
    gain_par = jnp.transpose(all_gain.reshape(-1, half_deg, 2), (2, 0, 1))
    own_modes = lax.dynamic_slice_in_dim(
        modes.reshape(-1), (chan_index * n_lat + lat_index) * per_dev, per_dev, 0
    )
    rows_x = folded.shape[2] * folded.shape[3] * folded.shape[4]
    gain_rows = jnp.tile(gain_par, (1, rows_x // gain_par.shape[1], 1))
    base = (chan_index * per_dev).astype(jnp.int32).reshape(1)
    back = legendre_stage(
        folded.reshape(per_dev, 2, rows_x, -1), legendre, gain_rows, own_modes, base
    )
    spread = pl.pallas_call(
        functools.partial(scatter_kernel, piece=piece, per_dev=per_dev, fields=fields),
        out_shape=jax.ShapeDtypeStruct((n_chan, 2 * per_dev, n_lat, row_count), jnp.bfloat16),
        compiler_params=pltpu.CompilerParams(vmem_limit_bytes=48 * 1024 * 1024),
    )(back)
    leaving = jnp.transpose(spread, (0, 2, 1, 3)).reshape(devices, 2 * per_dev, row_count)
    returned = lax.all_to_all(leaving, ("chan", "lat"), 0, 0, tiled=True)
    returned = returned.reshape(2 * total_modes, row_count)

    waveform = lax.dot_general(
        returned, inv, (((0,), (0,)), ((), ())), preferred_element_type=jnp.float32
    ) * ratio
    waveform = jnp.transpose(waveform.reshape(fields, 2, chans, cycles, period), (2, 0, 1, 3, 4))
    waveform = waveform.reshape(chans, fields, -1, period)
    primal_h = waveform[:, 0]
    sigmoid_h = jax.nn.sigmoid(primal_h)
    slope_h = sigmoid_h * (1.0 + primal_h * (1.0 - sigmoid_h))
    gain_h = primal_h * sigmoid_h
    flat = field.reshape(chans, fields, -1, points)
    pieces = []
    for n in range(points // period):
        initial = flat[:, :, :, n * period : (n + 1) * period].astype(jnp.float32)
        primal = initial[:, 0] + gain_h
        tangents = initial[:, 1:] + slope_h[:, None] * waveform[:, 1:]
        pieces.append(jnp.concatenate([primal[:, None], tangents], axis=1).astype(jnp.bfloat16))
    out = jnp.concatenate(pieces, axis=3)
    return out.reshape(field.shape)


def solution(mesh):
    n_lat = mesh.shape["lat"]
    n_chan = mesh.shape["chan"]
    placed = (
        P("chan", None, None, "lat", None),
        P(),
        P("chan", None),
        P(None, "lat", None, None),
        P(),
    )

    def body(field, mix_weight, spectral_gain, legendre, slot_mode):
        return local(field, mix_weight, spectral_gain, legendre, slot_mode, n_lat, n_chan)

    return jax.shard_map(
        body,
        mesh=mesh,
        in_specs=placed,
        out_specs=P("chan", None, None, "lat", None),
        check_vma=False,
    )
```

```python
import functools
import math

import jax
import jax.numpy as jnp
from jax import lax
from jax.experimental import pallas as pl
from jax.experimental.pallas import tpu as pltpu
from jax.sharding import PartitionSpec as P


def block_swap(x, piece):
    group, width = x.shape[1], x.shape[2]
    row = lax.broadcasted_iota(jnp.int32, x.shape, 1)
    blk = lax.broadcasted_iota(jnp.int32, x.shape, 2) // piece
    out = jnp.where(blk == row, x, 0.0)
    for d in range(1, group):
        moved = pltpu.roll(x, (-piece * d) % width, 2)
        moved = jnp.where(blk == row, moved, 0.0)
        out = out + pltpu.roll(moved, d, 1)
    return out


def tiles_of(x, group):
    return jnp.stack(
        [
            x[i * group : (i + 1) * group, j * 128 : (j + 1) * 128]
            for i in range(x.shape[0] // group)
            for j in range(x.shape[1] // 128)
        ]
    )


def gather_kernel(got_ref, mix_ref, out_ref, stage_ref, *, piece, per_dev, pairs):
    n_chan = got_ref.shape[0]
    lat_rows = got_ref.shape[2]
    group = 128 // piece

    def one(qs, carry):
        for c in range(n_chan):
            swapped = block_swap(tiles_of(got_ref[c, qs].astype(jnp.float32), group), piece)
            for tile in range(lat_rows // group):
                for th in range(pairs):
                    stage_ref[qs, th // 2, c, th % 2, :, tile * 128 : (tile + 1) * 128] = swapped[
                        tile * pairs + th
                    ]
        q = qs // per_dev
        s = qs % per_dev
        for t in range(pairs // 2):
            block = stage_ref[qs, t]
            block = block.reshape(-1, block.shape[-1]).astype(jnp.bfloat16)
            mixed = jnp.dot(mix_ref[...], block, preferred_element_type=jnp.float32)
            half = mixed.shape[0] // 2
            for p in range(2):
                out_ref[s, p, t, q] = mixed[p * half : (p + 1) * half].astype(out_ref.dtype)
        return carry

    lax.fori_loop(0, got_ref.shape[1], one, 0)


def scatter_kernel(back_ref, out_ref, *, piece, per_dev, fields):
    n_chan = out_ref.shape[0]
    lat_rows = out_ref.shape[2]
    group = 128 // piece
    chans = back_ref.shape[2] // (fields * 2)

    def one(qs, carry):
        q = qs // per_dev
        s = qs % per_dev
        for t in range(fields):
            for h in range(2):
                start = (t * 2 + q) * chans
                part = back_ref[s, h, pl.ds(pl.multiple_of(start, 8), chans)].astype(jnp.float32)
                swapped = block_swap(tiles_of(part, group), piece)
                th = t * 2 + h
                lane_tiles = part.shape[1] // 128
                for c in range(n_chan):
                    column = jnp.concatenate(
                        [swapped[c * lane_tiles + tile] for tile in range(lat_rows // group)], axis=0
                    )
                    out_ref[c, qs, :, th * 128 : (th + 1) * 128] = column.astype(out_ref.dtype)
        return carry

    lax.fori_loop(0, out_ref.shape[1], one, 0)


def legendre_kernel(modes_ref, base_ref, folded_ref, leg_ref, gain_ref, out_ref, *, block):
    s = pl.program_id(0)
    mode = modes_ref[s]
    half_deg = leg_ref.shape[-1]
    rows = folded_ref.shape[-2]
    north = folded_ref.shape[-1]
    syn = []
    for p in range(2):
        lhs = folded_ref[0, p]
        acc = jnp.zeros((north, rows), jnp.float32)
        for b in range(half_deg // block):
            def step(acc, p=p, b=b):
                table = leg_ref[p, 0, :, b * block : (b + 1) * block]
                coef = jnp.dot(lhs, table, preferred_element_type=jnp.float32)
                degree = 2 * (b * block + lax.broadcasted_iota(jnp.int32, (1, block), 1)) + p
                kept = jnp.where(
                    degree >= mode, gain_ref[p, :, b * block : (b + 1) * block] * coef, 0.0
                ).astype(jnp.bfloat16)
                return acc + jnp.dot(table, kept.T, preferred_element_type=jnp.float32)
            top = 2 * ((b + 1) * block - 1) + p
            acc = lax.cond(top >= mode, step, lambda a: a, acc)
        syn.append(acc)
    out_ref[0, 0] = (syn[0] + syn[1]).T.astype(out_ref.dtype)
    out_ref[0, 1] = (syn[0] - syn[1]).T.astype(out_ref.dtype)


def legendre_stage(folded, legendre, gain_rows, own_modes, base, block=256):
    per_dev, _, rows, north = folded.shape
    half_deg = legendre.shape[-1]
    grid_spec = pltpu.PrefetchScalarGridSpec(
        num_scalar_prefetch=2,
        grid=(per_dev,),
        in_specs=[
            pl.BlockSpec((1, 2, rows, north), lambda s, m, b: (s, 0, 0, 0)),
            pl.BlockSpec((2, 1, north, half_deg), lambda s, m, b: (0, b[0] + s, 0, 0)),
            pl.BlockSpec((2, rows, half_deg), lambda s, m, b: (0, 0, 0)),
        ],
        out_specs=pl.BlockSpec((1, 2, rows, north), lambda s, m, b: (s, 0, 0, 0)),
    )
    flops = 8 * per_dev * rows * north * half_deg
    return pl.pallas_call(
        functools.partial(legendre_kernel, block=block),
        grid_spec=grid_spec,
        out_shape=jax.ShapeDtypeStruct((per_dev, 2, rows, north), jnp.bfloat16),
        compiler_params=pltpu.CompilerParams(vmem_limit_bytes=48 * 1024 * 1024),
        cost_estimate=pl.CostEstimate(
            flops=flops, transcendentals=0,
            bytes_accessed=2 * per_dev * north * half_deg * 2 + 4 * folded.size + 4 * gain_rows.size,
        ),
    )(own_modes, base, folded, legendre, gain_rows)


def local(field, mix_weight, spectral_gain, legendre, slot_mode, n_lat, n_chan):
    chans = field.shape[0]
    fields = field.shape[1]
    cycles = field.shape[3]
    points = field.shape[4]
    total_modes = slot_mode.shape[0]
    degrees = spectral_gain.shape[1]
    half_deg = degrees // 2
    step_size = degrees // total_modes
    period = points // math.gcd(points, step_size)
    devices = n_lat * n_chan
    per_dev = total_modes // devices
    lat_index = lax.axis_index("lat")
    chan_index = lax.axis_index("chan")
    row_count = chans * fields * 2 * cycles

    modes = (slot_mode * step_size).reshape(n_lat, n_chan, per_dev)
    modes = jnp.transpose(modes, (1, 0, 2)).reshape(devices, 1, per_dev)
    quarter = jnp.array([0, points // 4], jnp.int32).reshape(1, 2, 1)
    lanes = min(128, period)
    blocks = period // lanes
    scale = 2.0 * math.pi / points
    hi_turns = (modes[..., None] * (lax.iota(jnp.int32, blocks) * lanes) + quarter[..., None]) % points
    lo_turns = (modes[..., None] * lax.iota(jnp.int32, lanes)) % points
    hi_angle = hi_turns.astype(jnp.float32) * scale
    lo_angle = lo_turns.astype(jnp.float32) * scale
    ca, sa = jnp.cos(hi_angle)[..., None], jnp.sin(hi_angle)[..., None]
    cb, sb = jnp.cos(lo_angle)[..., None, :], jnp.sin(lo_angle)[..., None, :]
    basis = (ca * cb - sa * sb).reshape(-1, period)
    fwd = (basis * math.sqrt(2.0 / points)).astype(jnp.bfloat16)
    ratio = math.sqrt(points / (2.0 * total_modes))
    if ratio == 2.0 ** round(math.log2(ratio)):
        fwd = lax.optimization_barrier(fwd)
        inv = fwd
    else:
        inv = (basis * math.sqrt(1.0 / total_modes)).astype(jnp.bfloat16)
        ratio = 1.0

    flat = jnp.transpose(field, (1, 2, 0, 3, 4)).reshape(-1, points)
    summed = flat[:, :period].astype(jnp.float32)
    for n in range(1, points // period):
        summed = summed + flat[:, n * period : (n + 1) * period].astype(jnp.float32)
    high = summed.astype(jnp.bfloat16)
    low = (summed - high.astype(jnp.float32)).astype(jnp.bfloat16)
    rows = jnp.concatenate([high, low], axis=1)
    spec_t = lax.dot_general(
        jnp.concatenate([fwd, fwd], axis=1), rows, (((1,), (1,)), ((), ())),
        preferred_element_type=jnp.float32,
    ).astype(jnp.bfloat16)

    sent = spec_t.reshape(devices, 2 * per_dev, row_count)
    got = lax.all_to_all(sent, ("chan", "lat"), 0, 0, tiled=True)
    got = jnp.transpose(got.reshape(n_chan, n_lat, 2 * per_dev, row_count), (0, 2, 1, 3))
    sign = jnp.array([[1.0, 1.0], [1.0, -1.0]], jnp.float32)
    weight = mix_weight.astype(jnp.float32).reshape(-1, n_chan, chans)
    mix_fold = sign[:, None, None, :, None] * weight[None, :, :, None, :]
    mix_fold = mix_fold.reshape(2 * weight.shape[0], -1).astype(jnp.bfloat16)
    piece = cycles
    folded = pl.pallas_call(
        functools.partial(gather_kernel, piece=piece, per_dev=per_dev, pairs=2 * fields),
        out_shape=jax.ShapeDtypeStruct(
            (per_dev, 2, fields, 2, weight.shape[0], n_lat * cycles), jnp.bfloat16
        ),
        scratch_shapes=[pltpu.VMEM((2 * per_dev, fields, n_chan, 2, chans, n_lat * cycles), jnp.float32)],
        compiler_params=pltpu.CompilerParams(vmem_limit_bytes=48 * 1024 * 1024),
    )(got, mix_fold)

    all_gain = lax.all_gather(spectral_gain, "chan", axis=0, tiled=True)
    gain_par = jnp.transpose(all_gain.reshape(-1, half_deg, 2), (2, 0, 1))
    own_modes = lax.dynamic_slice_in_dim(
        modes.reshape(-1), (chan_index * n_lat + lat_index) * per_dev, per_dev, 0
    )
    rows_x = folded.shape[2] * folded.shape[3] * folded.shape[4]
    gain_rows = jnp.tile(gain_par, (1, rows_x // gain_par.shape[1], 1))
    base = (chan_index * per_dev).astype(jnp.int32).reshape(1)
    back = legendre_stage(
        folded.reshape(per_dev, 2, rows_x, -1), legendre, gain_rows, own_modes, base
    )
    spread = pl.pallas_call(
        functools.partial(scatter_kernel, piece=piece, per_dev=per_dev, fields=fields),
        out_shape=jax.ShapeDtypeStruct((n_chan, 2 * per_dev, n_lat, row_count), jnp.bfloat16),
        compiler_params=pltpu.CompilerParams(vmem_limit_bytes=48 * 1024 * 1024),
    )(back)
    leaving = jnp.transpose(spread, (0, 2, 1, 3)).reshape(devices, 2 * per_dev, row_count)
    returned = lax.all_to_all(leaving, ("chan", "lat"), 0, 0, tiled=True)
    returned = returned.reshape(2 * total_modes, row_count)

    waveform = lax.dot_general(
        returned, inv, (((0,), (0,)), ((), ())), preferred_element_type=jnp.float32
    ) * ratio
    waveform = jnp.transpose(waveform.reshape(fields, 2, chans, cycles, period), (2, 0, 1, 3, 4))
    waveform = waveform.reshape(chans, fields, -1, period)
    primal_h = waveform[:, 0]
    sigmoid_h = jax.nn.sigmoid(primal_h)
    slope_h = sigmoid_h * (1.0 + primal_h * (1.0 - sigmoid_h))
    gain_h = primal_h * sigmoid_h
    flat = field.reshape(chans, fields, -1, points)
    pieces = []
    for n in range(points // period):
        initial = flat[:, :, :, n * period : (n + 1) * period].astype(jnp.float32)
        primal = initial[:, 0] + gain_h
        tangents = initial[:, 1:] + slope_h[:, None] * waveform[:, 1:]
        pieces.append(jnp.concatenate([primal[:, None], tangents], axis=1).astype(jnp.bfloat16))
    out = jnp.concatenate(pieces, axis=3)
    return out.reshape(field.shape)


def solution(mesh):
    n_lat = mesh.shape["lat"]
    n_chan = mesh.shape["chan"]
    placed = (
        P("chan", None, None, "lat", None),
        P(),
        P("chan", None),
        P(None, "lat", None, None),
        P(),
    )

    def body(field, mix_weight, spectral_gain, legendre, slot_mode):
        return local(field, mix_weight, spectral_gain, legendre, slot_mode, n_lat, n_chan)

    return jax.shard_map(
        body,
        mesh=mesh,
        in_specs=placed,
        out_specs=P("chan", None, None, "lat", None),
        check_vma=False,
    )
```

```python
import functools
import math

import jax
import jax.numpy as jnp
from jax import lax
from jax.experimental import pallas as pl
from jax.experimental.pallas import tpu as pltpu
from jax.sharding import PartitionSpec as P


def block_swap(x, piece):
    group, width = x.shape[1], x.shape[2]
    row = lax.broadcasted_iota(jnp.int32, x.shape, 1)
    blk = lax.broadcasted_iota(jnp.int32, x.shape, 2) // piece
    out = jnp.where(blk == row, x, 0.0)
    for d in range(1, group):
        moved = pltpu.roll(x, (-piece * d) % width, 2)
        moved = jnp.where(blk == row, moved, 0.0)
        out = out + pltpu.roll(moved, d, 1)
    return out


def tiles_of(x, group):
    return jnp.stack(
        [
            x[i * group : (i + 1) * group, j * 128 : (j + 1) * 128]
            for i in range(x.shape[0] // group)
            for j in range(x.shape[1] // 128)
        ]
    )


def gather_kernel(got_ref, mix_ref, out_ref, stage_ref, *, piece, per_dev, pairs):
    n_chan = got_ref.shape[0]
    lat_rows = got_ref.shape[2]
    group = 128 // piece

    def one(qs, carry):
        for c in range(n_chan):
            swapped = block_swap(tiles_of(got_ref[c, qs].astype(jnp.float32), group), piece)
            for tile in range(lat_rows // group):
                for th in range(pairs):
                    stage_ref[qs, th // 2, c, th % 2, :, tile * 128 : (tile + 1) * 128] = swapped[
                        tile * pairs + th
                    ]
        q = qs // per_dev
        s = qs % per_dev
        for t in range(pairs // 2):
            block = stage_ref[qs, t]
            block = block.reshape(-1, block.shape[-1]).astype(jnp.bfloat16)
            mixed = jnp.dot(mix_ref[...], block, preferred_element_type=jnp.float32)
            half = mixed.shape[0] // 2
            for p in range(2):
                out_ref[s, p, t, q] = mixed[p * half : (p + 1) * half].astype(out_ref.dtype)
        return carry

    lax.fori_loop(0, got_ref.shape[1], one, 0)


def scatter_kernel(back_ref, out_ref, *, piece, per_dev, fields):
    n_chan = out_ref.shape[0]
    lat_rows = out_ref.shape[2]
    group = 128 // piece
    chans = back_ref.shape[2] // (fields * 2)

    def one(qs, carry):
        q = qs // per_dev
        s = qs % per_dev
        for t in range(fields):
            for h in range(2):
                start = (t * 2 + q) * chans
                part = back_ref[s, h, pl.ds(pl.multiple_of(start, 8), chans)].astype(jnp.float32)
                swapped = block_swap(tiles_of(part, group), piece)
                th = t * 2 + h
                lane_tiles = part.shape[1] // 128
                for c in range(n_chan):
                    column = jnp.concatenate(
                        [swapped[c * lane_tiles + tile] for tile in range(lat_rows // group)], axis=0
                    )
                    out_ref[c, qs, :, th * 128 : (th + 1) * 128] = column.astype(out_ref.dtype)
        return carry

    lax.fori_loop(0, out_ref.shape[1], one, 0)


def legendre_kernel(modes_ref, base_ref, folded_ref, leg_ref, gain_ref, out_ref, *, block):
    s = pl.program_id(0)
    mode = modes_ref[s]
    half_deg = leg_ref.shape[-1]
    rows = folded_ref.shape[-2]
    north = folded_ref.shape[-1]
    syn = []
    for p in range(2):
        lhs = folded_ref[0, p]
        acc = jnp.zeros((rows, north), jnp.float32)
        for b in range(half_deg // block):
            def step(acc, p=p, b=b):
                table = leg_ref[p, 0, :, b * block : (b + 1) * block]
                coef = jnp.dot(lhs, table, preferred_element_type=jnp.float32)
                degree = 2 * (b * block + lax.broadcasted_iota(jnp.int32, (1, block), 1)) + p
                kept = jnp.where(
                    degree >= mode, gain_ref[p, :, b * block : (b + 1) * block] * coef, 0.0
                ).astype(jnp.bfloat16)
                return acc + lax.dot_general(
                    kept, table, (((1,), (1,)), ((), ())), preferred_element_type=jnp.float32
                )
            top = 2 * ((b + 1) * block - 1) + p
            acc = lax.cond(top >= mode, step, lambda a: a, acc)
        syn.append(acc)
    out_ref[0, 0] = (syn[0] + syn[1]).astype(out_ref.dtype)
    out_ref[0, 1] = (syn[0] - syn[1]).astype(out_ref.dtype)


def legendre_stage(folded, legendre, gain_rows, own_modes, base, block=512):
    per_dev, _, rows, north = folded.shape
    half_deg = legendre.shape[-1]
    grid_spec = pltpu.PrefetchScalarGridSpec(
        num_scalar_prefetch=2,
        grid=(per_dev,),
        in_specs=[
            pl.BlockSpec((1, 2, rows, north), lambda s, m, b: (s, 0, 0, 0)),
            pl.BlockSpec((2, 1, north, half_deg), lambda s, m, b: (0, b[0] + s, 0, 0)),
            pl.BlockSpec((2, rows, half_deg), lambda s, m, b: (0, 0, 0)),
        ],
        out_specs=pl.BlockSpec((1, 2, rows, north), lambda s, m, b: (s, 0, 0, 0)),
    )
    flops = 8 * per_dev * rows * north * half_deg
    return pl.pallas_call(
        functools.partial(legendre_kernel, block=block),
        grid_spec=grid_spec,
        out_shape=jax.ShapeDtypeStruct((per_dev, 2, rows, north), jnp.bfloat16),
        compiler_params=pltpu.CompilerParams(vmem_limit_bytes=48 * 1024 * 1024),
        cost_estimate=pl.CostEstimate(
            flops=flops, transcendentals=0,
            bytes_accessed=2 * per_dev * north * half_deg * 2 + 4 * folded.size + 4 * gain_rows.size,
        ),
    )(own_modes, base, folded, legendre, gain_rows)


def local(field, mix_weight, spectral_gain, legendre, slot_mode, n_lat, n_chan):
    chans = field.shape[0]
    fields = field.shape[1]
    cycles = field.shape[3]
    points = field.shape[4]
    total_modes = slot_mode.shape[0]
    degrees = spectral_gain.shape[1]
    half_deg = degrees // 2
    step_size = degrees // total_modes
    period = points // math.gcd(points, step_size)
    devices = n_lat * n_chan
    per_dev = total_modes // devices
    lat_index = lax.axis_index("lat")
    chan_index = lax.axis_index("chan")
    row_count = chans * fields * 2 * cycles

    modes = (slot_mode * step_size).reshape(n_lat, n_chan, per_dev)
    modes = jnp.transpose(modes, (1, 0, 2)).reshape(devices, 1, per_dev)
    quarter = jnp.array([0, points // 4], jnp.int32).reshape(1, 2, 1)
    lanes = min(128, period)
    blocks = period // lanes
    scale = 2.0 * math.pi / points
    hi_turns = (modes[..., None] * (lax.iota(jnp.int32, blocks) * lanes) + quarter[..., None]) % points
    lo_turns = (modes[..., None] * lax.iota(jnp.int32, lanes)) % points
    hi_angle = hi_turns.astype(jnp.float32) * scale
    lo_angle = lo_turns.astype(jnp.float32) * scale
    ca, sa = jnp.cos(hi_angle)[..., None], jnp.sin(hi_angle)[..., None]
    cb, sb = jnp.cos(lo_angle)[..., None, :], jnp.sin(lo_angle)[..., None, :]
    basis = (ca * cb - sa * sb).reshape(-1, period)
    fwd = (basis * math.sqrt(2.0 / points)).astype(jnp.bfloat16)
    ratio = math.sqrt(points / (2.0 * total_modes))
    if ratio == 2.0 ** round(math.log2(ratio)):
        fwd = lax.optimization_barrier(fwd)
        inv = fwd
    else:
        inv = (basis * math.sqrt(1.0 / total_modes)).astype(jnp.bfloat16)
        ratio = 1.0

    flat = jnp.transpose(field, (1, 2, 0, 3, 4)).reshape(-1, points)
    summed = flat[:, :period].astype(jnp.float32)
    for n in range(1, points // period):
        summed = summed + flat[:, n * period : (n + 1) * period].astype(jnp.float32)
    high = summed.astype(jnp.bfloat16)
    low = (summed - high.astype(jnp.float32)).astype(jnp.bfloat16)
    rows = jnp.concatenate([high, low], axis=1)
    spec_t = lax.dot_general(
        jnp.concatenate([fwd, fwd], axis=1), rows, (((1,), (1,)), ((), ())),
        preferred_element_type=jnp.float32,
    ).astype(jnp.bfloat16)

    sent = spec_t.reshape(devices, 2 * per_dev, row_count)
    got = lax.all_to_all(sent, ("chan", "lat"), 0, 0, tiled=True)
    got = jnp.transpose(got.reshape(n_chan, n_lat, 2 * per_dev, row_count), (0, 2, 1, 3))
    sign = jnp.array([[1.0, 1.0], [1.0, -1.0]], jnp.float32)
    weight = mix_weight.astype(jnp.float32).reshape(-1, n_chan, chans)
    mix_fold = sign[:, None, None, :, None] * weight[None, :, :, None, :]
    mix_fold = mix_fold.reshape(2 * weight.shape[0], -1).astype(jnp.bfloat16)
    piece = cycles
    folded = pl.pallas_call(
        functools.partial(gather_kernel, piece=piece, per_dev=per_dev, pairs=2 * fields),
        out_shape=jax.ShapeDtypeStruct(
            (per_dev, 2, fields, 2, weight.shape[0], n_lat * cycles), jnp.bfloat16
        ),
        scratch_shapes=[pltpu.VMEM((2 * per_dev, fields, n_chan, 2, chans, n_lat * cycles), jnp.float32)],
        compiler_params=pltpu.CompilerParams(vmem_limit_bytes=48 * 1024 * 1024),
    )(got, mix_fold)

    all_gain = lax.all_gather(spectral_gain, "chan", axis=0, tiled=True)
    gain_par = jnp.transpose(all_gain.reshape(-1, half_deg, 2), (2, 0, 1))
    own_modes = lax.dynamic_slice_in_dim(
        modes.reshape(-1), (chan_index * n_lat + lat_index) * per_dev, per_dev, 0
    )
    rows_x = folded.shape[2] * folded.shape[3] * folded.shape[4]
    gain_rows = jnp.tile(gain_par, (1, rows_x // gain_par.shape[1], 1))
    base = (chan_index * per_dev).astype(jnp.int32).reshape(1)
    back = legendre_stage(
        folded.reshape(per_dev, 2, rows_x, -1), legendre, gain_rows, own_modes, base
    )
    spread = pl.pallas_call(
        functools.partial(scatter_kernel, piece=piece, per_dev=per_dev, fields=fields),
        out_shape=jax.ShapeDtypeStruct((n_chan, 2 * per_dev, n_lat, row_count), jnp.bfloat16),
        compiler_params=pltpu.CompilerParams(vmem_limit_bytes=48 * 1024 * 1024),
    )(back)
    leaving = jnp.transpose(spread, (0, 2, 1, 3)).reshape(devices, 2 * per_dev, row_count)
    returned = lax.all_to_all(leaving, ("chan", "lat"), 0, 0, tiled=True)
    returned = returned.reshape(2 * total_modes, row_count)

    waveform = lax.dot_general(
        returned, inv, (((0,), (0,)), ((), ())), preferred_element_type=jnp.float32
    ) * ratio
    waveform = jnp.transpose(waveform.reshape(fields, 2, chans, cycles, period), (2, 0, 1, 3, 4))
    waveform = waveform.reshape(chans, fields, -1, period)
    primal_h = waveform[:, 0]
    sigmoid_h = jax.nn.sigmoid(primal_h)
    slope_h = sigmoid_h * (1.0 + primal_h * (1.0 - sigmoid_h))
    gain_h = primal_h * sigmoid_h
    flat = field.reshape(chans, fields, -1, points)
    pieces = []
    for n in range(points // period):
        initial = flat[:, :, :, n * period : (n + 1) * period].astype(jnp.float32)
        primal = initial[:, 0] + gain_h
        tangents = initial[:, 1:] + slope_h[:, None] * waveform[:, 1:]
        pieces.append(jnp.concatenate([primal[:, None], tangents], axis=1).astype(jnp.bfloat16))
    out = jnp.concatenate(pieces, axis=3)
    return out.reshape(field.shape)


def solution(mesh):
    n_lat = mesh.shape["lat"]
    n_chan = mesh.shape["chan"]
    placed = (
        P("chan", None, None, "lat", None),
        P(),
        P("chan", None),
        P(None, "lat", None, None),
        P(),
    )

    def body(field, mix_weight, spectral_gain, legendre, slot_mode):
        return local(field, mix_weight, spectral_gain, legendre, slot_mode, n_lat, n_chan)

    return jax.shard_map(
        body,
        mesh=mesh,
        in_specs=placed,
        out_specs=P("chan", None, None, "lat", None),
        check_vma=False,
    )
```

```python
import functools
import math

import jax
import jax.numpy as jnp
from jax import lax
from jax.experimental import pallas as pl
from jax.experimental.pallas import tpu as pltpu
from jax.sharding import PartitionSpec as P


def block_swap(x, piece):
    group, width = x.shape[1], x.shape[2]
    row = lax.broadcasted_iota(jnp.int32, x.shape, 1)
    blk = lax.broadcasted_iota(jnp.int32, x.shape, 2) // piece
    out = jnp.where(blk == row, x, 0.0)
    for d in range(1, group):
        moved = pltpu.roll(x, (-piece * d) % width, 2)
        moved = jnp.where(blk == row, moved, 0.0)
        out = out + pltpu.roll(moved, d, 1)
    return out


def tiles_of(x, group):
    return jnp.stack(
        [
            x[i * group : (i + 1) * group, j * 128 : (j + 1) * 128]
            for i in range(x.shape[0] // group)
            for j in range(x.shape[1] // 128)
        ]
    )


def gather_kernel(got_ref, mix_ref, out_ref, stage_ref, *, piece, per_dev, pairs):
    n_chan = got_ref.shape[0]
    lat_rows = got_ref.shape[2]
    group = 128 // piece

    def one(qs, carry):
        for c in range(n_chan):
            swapped = block_swap(tiles_of(got_ref[c, qs].astype(jnp.float32), group), piece)
            for tile in range(lat_rows // group):
                for th in range(pairs):
                    stage_ref[qs, th // 2, c, th % 2, :, tile * 128 : (tile + 1) * 128] = swapped[
                        tile * pairs + th
                    ]
        q = qs // per_dev
        s = qs % per_dev
        for t in range(pairs // 2):
            block = stage_ref[qs, t]
            block = block.reshape(-1, block.shape[-1]).astype(jnp.bfloat16)
            mixed = jnp.dot(mix_ref[...], block, preferred_element_type=jnp.float32)
            half = mixed.shape[0] // 2
            for p in range(2):
                out_ref[s, p, t, q] = mixed[p * half : (p + 1) * half].astype(out_ref.dtype)
        return carry

    lax.fori_loop(0, got_ref.shape[1], one, 0)


def scatter_kernel(back_ref, out_ref, *, piece, per_dev, fields):
    n_chan = out_ref.shape[0]
    lat_rows = out_ref.shape[2]
    group = 128 // piece
    chans = back_ref.shape[2] // (fields * 2)

    def one(qs, carry):
        q = qs // per_dev
        s = qs % per_dev
        for t in range(fields):
            for h in range(2):
                start = (t * 2 + q) * chans
                part = back_ref[s, h, pl.ds(pl.multiple_of(start, 8), chans)].astype(jnp.float32)
                swapped = block_swap(tiles_of(part, group), piece)
                th = t * 2 + h
                lane_tiles = part.shape[1] // 128
                for c in range(n_chan):
                    column = jnp.concatenate(
                        [swapped[c * lane_tiles + tile] for tile in range(lat_rows // group)], axis=0
                    )
                    out_ref[c, qs, :, th * 128 : (th + 1) * 128] = column.astype(out_ref.dtype)
        return carry

    lax.fori_loop(0, out_ref.shape[1], one, 0)


def legendre_kernel(modes_ref, base_ref, folded_ref, leg_ref, gain_ref, out_ref, *, block):
    s = pl.program_id(0)
    mode = modes_ref[s]
    half_deg = leg_ref.shape[-1]
    rows = folded_ref.shape[-2]
    north = folded_ref.shape[-1]
    syn = []
    for p in range(2):
        lhs = folded_ref[0, p]
        acc = jnp.zeros((rows, north), jnp.float32)
        for b in range(half_deg // block):
            def step(acc, p=p, b=b):
                table = leg_ref[p, 0, :, b * block : (b + 1) * block]
                coef = jnp.dot(lhs, table, preferred_element_type=jnp.float32)
                degree = 2 * (b * block + lax.broadcasted_iota(jnp.int32, (1, block), 1)) + p
                kept = jnp.where(
                    degree >= mode, gain_ref[p, :, b * block : (b + 1) * block] * coef, 0.0
                ).astype(jnp.bfloat16)
                return acc + lax.dot_general(
                    kept, table, (((1,), (1,)), ((), ())), preferred_element_type=jnp.float32
                )
            top = 2 * ((b + 1) * block - 1) + p
            acc = lax.cond(top >= mode, step, lambda a: a, acc)
        syn.append(acc)
    out_ref[0, 0] = (syn[0] + syn[1]).astype(out_ref.dtype)
    out_ref[0, 1] = (syn[0] - syn[1]).astype(out_ref.dtype)


def legendre_stage(folded, legendre, gain_rows, own_modes, base, block=1024):
    per_dev, _, rows, north = folded.shape
    half_deg = legendre.shape[-1]
    grid_spec = pltpu.PrefetchScalarGridSpec(
        num_scalar_prefetch=2,
        grid=(per_dev,),
        in_specs=[
            pl.BlockSpec((1, 2, rows, north), lambda s, m, b: (s, 0, 0, 0)),
            pl.BlockSpec((2, 1, north, half_deg), lambda s, m, b: (0, b[0] + s, 0, 0)),
            pl.BlockSpec((2, rows, half_deg), lambda s, m, b: (0, 0, 0)),
        ],
        out_specs=pl.BlockSpec((1, 2, rows, north), lambda s, m, b: (s, 0, 0, 0)),
    )
    flops = 8 * per_dev * rows * north * half_deg
    return pl.pallas_call(
        functools.partial(legendre_kernel, block=block),
        grid_spec=grid_spec,
        out_shape=jax.ShapeDtypeStruct((per_dev, 2, rows, north), jnp.bfloat16),
        compiler_params=pltpu.CompilerParams(vmem_limit_bytes=48 * 1024 * 1024),
        cost_estimate=pl.CostEstimate(
            flops=flops, transcendentals=0,
            bytes_accessed=2 * per_dev * north * half_deg * 2 + 4 * folded.size + 4 * gain_rows.size,
        ),
    )(own_modes, base, folded, legendre, gain_rows)


def local(field, mix_weight, spectral_gain, legendre, slot_mode, n_lat, n_chan):
    chans = field.shape[0]
    fields = field.shape[1]
    cycles = field.shape[3]
    points = field.shape[4]
    total_modes = slot_mode.shape[0]
    degrees = spectral_gain.shape[1]
    half_deg = degrees // 2
    step_size = degrees // total_modes
    period = points // math.gcd(points, step_size)
    devices = n_lat * n_chan
    per_dev = total_modes // devices
    lat_index = lax.axis_index("lat")
    chan_index = lax.axis_index("chan")
    row_count = chans * fields * 2 * cycles

    modes = (slot_mode * step_size).reshape(n_lat, n_chan, per_dev)
    modes = jnp.transpose(modes, (1, 0, 2)).reshape(devices, 1, per_dev)
    quarter = jnp.array([0, points // 4], jnp.int32).reshape(1, 2, 1)
    lanes = min(128, period)
    blocks = period // lanes
    scale = 2.0 * math.pi / points
    hi_turns = (modes[..., None] * (lax.iota(jnp.int32, blocks) * lanes) + quarter[..., None]) % points
    lo_turns = (modes[..., None] * lax.iota(jnp.int32, lanes)) % points
    hi_angle = hi_turns.astype(jnp.float32) * scale
    lo_angle = lo_turns.astype(jnp.float32) * scale
    ca, sa = jnp.cos(hi_angle)[..., None], jnp.sin(hi_angle)[..., None]
    cb, sb = jnp.cos(lo_angle)[..., None, :], jnp.sin(lo_angle)[..., None, :]
    basis = (ca * cb - sa * sb).reshape(-1, period)
    fwd = (basis * math.sqrt(2.0 / points)).astype(jnp.bfloat16)
    ratio = math.sqrt(points / (2.0 * total_modes))
    if ratio == 2.0 ** round(math.log2(ratio)):
        fwd = lax.optimization_barrier(fwd)
        inv = fwd
    else:
        inv = (basis * math.sqrt(1.0 / total_modes)).astype(jnp.bfloat16)
        ratio = 1.0

    flat = jnp.transpose(field, (1, 2, 0, 3, 4)).reshape(-1, points)
    summed = flat[:, :period].astype(jnp.float32)
    for n in range(1, points // period):
        summed = summed + flat[:, n * period : (n + 1) * period].astype(jnp.float32)
    high = summed.astype(jnp.bfloat16)
    low = (summed - high.astype(jnp.float32)).astype(jnp.bfloat16)
    rows = jnp.concatenate([high, low], axis=1)
    spec_t = lax.dot_general(
        jnp.concatenate([fwd, fwd], axis=1), rows, (((1,), (1,)), ((), ())),
        preferred_element_type=jnp.float32,
    ).astype(jnp.bfloat16)

    sent = spec_t.reshape(devices, 2 * per_dev, row_count)
    got = lax.all_to_all(sent, ("chan", "lat"), 0, 0, tiled=True)
    got = jnp.transpose(got.reshape(n_chan, n_lat, 2 * per_dev, row_count), (0, 2, 1, 3))
    sign = jnp.array([[1.0, 1.0], [1.0, -1.0]], jnp.float32)
    weight = mix_weight.astype(jnp.float32).reshape(-1, n_chan, chans)
    mix_fold = sign[:, None, None, :, None] * weight[None, :, :, None, :]
    mix_fold = mix_fold.reshape(2 * weight.shape[0], -1).astype(jnp.bfloat16)
    piece = cycles
    folded = pl.pallas_call(
        functools.partial(gather_kernel, piece=piece, per_dev=per_dev, pairs=2 * fields),
        out_shape=jax.ShapeDtypeStruct(
            (per_dev, 2, fields, 2, weight.shape[0], n_lat * cycles), jnp.bfloat16
        ),
        scratch_shapes=[pltpu.VMEM((2 * per_dev, fields, n_chan, 2, chans, n_lat * cycles), jnp.float32)],
        compiler_params=pltpu.CompilerParams(vmem_limit_bytes=48 * 1024 * 1024),
    )(got, mix_fold)

    all_gain = lax.all_gather(spectral_gain, "chan", axis=0, tiled=True)
    gain_par = jnp.transpose(all_gain.reshape(-1, half_deg, 2), (2, 0, 1))
    own_modes = lax.dynamic_slice_in_dim(
        modes.reshape(-1), (chan_index * n_lat + lat_index) * per_dev, per_dev, 0
    )
    rows_x = folded.shape[2] * folded.shape[3] * folded.shape[4]
    gain_rows = jnp.tile(gain_par, (1, rows_x // gain_par.shape[1], 1))
    base = (chan_index * per_dev).astype(jnp.int32).reshape(1)
    back = legendre_stage(
        folded.reshape(per_dev, 2, rows_x, -1), legendre, gain_rows, own_modes, base
    )
    spread = pl.pallas_call(
        functools.partial(scatter_kernel, piece=piece, per_dev=per_dev, fields=fields),
        out_shape=jax.ShapeDtypeStruct((n_chan, 2 * per_dev, n_lat, row_count), jnp.bfloat16),
        compiler_params=pltpu.CompilerParams(vmem_limit_bytes=48 * 1024 * 1024),
    )(back)
    leaving = jnp.transpose(spread, (0, 2, 1, 3)).reshape(devices, 2 * per_dev, row_count)
    returned = lax.all_to_all(leaving, ("chan", "lat"), 0, 0, tiled=True)
    returned = returned.reshape(2 * total_modes, row_count)

    waveform = lax.dot_general(
        returned, inv, (((0,), (0,)), ((), ())), preferred_element_type=jnp.float32
    ) * ratio
    waveform = jnp.transpose(waveform.reshape(fields, 2, chans, cycles, period), (2, 0, 1, 3, 4))
    waveform = waveform.reshape(chans, fields, -1, period)
    primal_h = waveform[:, 0]
    sigmoid_h = jax.nn.sigmoid(primal_h)
    slope_h = sigmoid_h * (1.0 + primal_h * (1.0 - sigmoid_h))
    gain_h = primal_h * sigmoid_h
    flat = field.reshape(chans, fields, -1, points)
    pieces = []
    for n in range(points // period):
        initial = flat[:, :, :, n * period : (n + 1) * period].astype(jnp.float32)
        primal = initial[:, 0] + gain_h
        tangents = initial[:, 1:] + slope_h[:, None] * waveform[:, 1:]
        pieces.append(jnp.concatenate([primal[:, None], tangents], axis=1).astype(jnp.bfloat16))
    out = jnp.concatenate(pieces, axis=3)
    return out.reshape(field.shape)


def solution(mesh):
    n_lat = mesh.shape["lat"]
    n_chan = mesh.shape["chan"]
    placed = (
        P("chan", None, None, "lat", None),
        P(),
        P("chan", None),
        P(None, "lat", None, None),
        P(),
    )

    def body(field, mix_weight, spectral_gain, legendre, slot_mode):
        return local(field, mix_weight, spectral_gain, legendre, slot_mode, n_lat, n_chan)

    return jax.shard_map(
        body,
        mesh=mesh,
        in_specs=placed,
        out_specs=P("chan", None, None, "lat", None),
        check_vma=False,
    )
```

```python
import functools
import math

import jax
import jax.numpy as jnp
from jax import lax
from jax.experimental import pallas as pl
from jax.experimental.pallas import tpu as pltpu
from jax.sharding import PartitionSpec as P


def block_swap(x, piece):
    group, width = x.shape[1], x.shape[2]
    row = lax.broadcasted_iota(jnp.int32, x.shape, 1)
    blk = lax.broadcasted_iota(jnp.int32, x.shape, 2) // piece
    out = jnp.where(blk == row, x, 0.0)
    for d in range(1, group):
        moved = pltpu.roll(x, (-piece * d) % width, 2)
        moved = jnp.where(blk == row, moved, 0.0)
        out = out + pltpu.roll(moved, d, 1)
    return out


def tiles_of(x, group):
    return jnp.stack(
        [
            x[i * group : (i + 1) * group, j * 128 : (j + 1) * 128]
            for i in range(x.shape[0] // group)
            for j in range(x.shape[1] // 128)
        ]
    )


def gather_kernel(got_ref, mix_ref, out_ref, stage_ref, *, piece, per_dev, pairs):
    n_chan = got_ref.shape[0]
    lat_rows = got_ref.shape[2]
    group = 128 // piece

    def one(qs, carry):
        for c in range(n_chan):
            swapped = block_swap(tiles_of(got_ref[c, qs].astype(jnp.float32), group), piece)
            for tile in range(lat_rows // group):
                for th in range(pairs):
                    stage_ref[qs, th // 2, c, th % 2, :, tile * 128 : (tile + 1) * 128] = swapped[
                        tile * pairs + th
                    ]
        q = qs // per_dev
        s = qs % per_dev
        for t in range(pairs // 2):
            block = stage_ref[qs, t]
            block = block.reshape(-1, block.shape[-1]).astype(jnp.bfloat16)
            mixed = jnp.dot(mix_ref[...], block, preferred_element_type=jnp.float32)
            half = mixed.shape[0] // 2
            for p in range(2):
                out_ref[s, p, t, q] = mixed[p * half : (p + 1) * half].astype(out_ref.dtype)
        return carry

    lax.fori_loop(0, got_ref.shape[1], one, 0)


def scatter_kernel(back_ref, out_ref, *, piece, per_dev, fields):
    n_chan = out_ref.shape[0]
    lat_rows = out_ref.shape[2]
    group = 128 // piece
    chans = back_ref.shape[2] // (fields * 2)

    def one(qs, carry):
        q = qs // per_dev
        s = qs % per_dev
        for t in range(fields):
            for h in range(2):
                start = (t * 2 + q) * chans
                part = back_ref[s, h, pl.ds(pl.multiple_of(start, 8), chans)].astype(jnp.float32)
                swapped = block_swap(tiles_of(part, group), piece)
                th = t * 2 + h
                lane_tiles = part.shape[1] // 128
                for c in range(n_chan):
                    column = jnp.concatenate(
                        [swapped[c * lane_tiles + tile] for tile in range(lat_rows // group)], axis=0
                    )
                    out_ref[c, qs, :, th * 128 : (th + 1) * 128] = column.astype(out_ref.dtype)
        return carry

    lax.fori_loop(0, out_ref.shape[1], one, 0)


def epilogue_kernel(wave_ref, field_ref, out_ref, *, period):
    fields = wave_ref.shape[0]
    primal_h = wave_ref[0, :, 0]
    sigmoid_h = 1.0 / (1.0 + jnp.exp(-primal_h))
    slope_h = sigmoid_h * (1.0 + primal_h * (1.0 - sigmoid_h))
    gain_h = primal_h * sigmoid_h
    for n in range(field_ref.shape[-1] // period):
        cols = slice(n * period, (n + 1) * period)
        out_ref[0, 0, :, :, cols] = (
            field_ref[0, 0, :, :, cols].astype(jnp.float32) + gain_h
        ).astype(out_ref.dtype)
        for t in range(1, fields):
            out_ref[0, t, :, :, cols] = (
                field_ref[0, t, :, :, cols].astype(jnp.float32) + slope_h * wave_ref[t, :, 0]
            ).astype(out_ref.dtype)


def legendre_kernel(modes_ref, base_ref, folded_ref, leg_ref, gain_ref, out_ref, *, block):
    s = pl.program_id(0)
    mode = modes_ref[s]
    half_deg = leg_ref.shape[-1]
    rows = folded_ref.shape[-2]
    north = folded_ref.shape[-1]
    syn = []
    for p in range(2):
        lhs = folded_ref[0, p]
        acc = jnp.zeros((rows, north), jnp.float32)
        for b in range(half_deg // block):
            def step(acc, p=p, b=b):
                table = leg_ref[p, 0, :, b * block : (b + 1) * block]
                coef = jnp.dot(lhs, table, preferred_element_type=jnp.float32)
                degree = 2 * (b * block + lax.broadcasted_iota(jnp.int32, (1, block), 1)) + p
                kept = jnp.where(
                    degree >= mode, gain_ref[p, :, b * block : (b + 1) * block] * coef, 0.0
                ).astype(jnp.bfloat16)
                return acc + lax.dot_general(
                    kept, table, (((1,), (1,)), ((), ())), preferred_element_type=jnp.float32
                )
            top = 2 * ((b + 1) * block - 1) + p
            acc = lax.cond(top >= mode, step, lambda a: a, acc)
        syn.append(acc)
    out_ref[0, 0] = (syn[0] + syn[1]).astype(out_ref.dtype)
    out_ref[0, 1] = (syn[0] - syn[1]).astype(out_ref.dtype)


def legendre_stage(folded, legendre, gain_rows, own_modes, base, block=1024):
    per_dev, _, rows, north = folded.shape
    half_deg = legendre.shape[-1]
    grid_spec = pltpu.PrefetchScalarGridSpec(
        num_scalar_prefetch=2,
        grid=(per_dev,),
        in_specs=[
            pl.BlockSpec((1, 2, rows, north), lambda s, m, b: (s, 0, 0, 0)),
            pl.BlockSpec((2, 1, north, half_deg), lambda s, m, b: (0, b[0] + s, 0, 0)),
            pl.BlockSpec((2, rows, half_deg), lambda s, m, b: (0, 0, 0)),
        ],
        out_specs=pl.BlockSpec((1, 2, rows, north), lambda s, m, b: (s, 0, 0, 0)),
    )
    flops = 8 * per_dev * rows * north * half_deg
    return pl.pallas_call(
        functools.partial(legendre_kernel, block=block),
        grid_spec=grid_spec,
        out_shape=jax.ShapeDtypeStruct((per_dev, 2, rows, north), jnp.bfloat16),
        compiler_params=pltpu.CompilerParams(vmem_limit_bytes=48 * 1024 * 1024),
        cost_estimate=pl.CostEstimate(
            flops=flops, transcendentals=0,
            bytes_accessed=2 * per_dev * north * half_deg * 2 + 4 * folded.size + 4 * gain_rows.size,
        ),
    )(own_modes, base, folded, legendre, gain_rows)


def local(field, mix_weight, spectral_gain, legendre, slot_mode, n_lat, n_chan):
    chans = field.shape[0]
    fields = field.shape[1]
    cycles = field.shape[3]
    points = field.shape[4]
    total_modes = slot_mode.shape[0]
    degrees = spectral_gain.shape[1]
    half_deg = degrees // 2
    step_size = degrees // total_modes
    period = points // math.gcd(points, step_size)
    devices = n_lat * n_chan
    per_dev = total_modes // devices
    lat_index = lax.axis_index("lat")
    chan_index = lax.axis_index("chan")
    row_count = chans * fields * 2 * cycles

    modes = (slot_mode * step_size).reshape(n_lat, n_chan, per_dev)
    modes = jnp.transpose(modes, (1, 0, 2)).reshape(devices, 1, per_dev)
    quarter = jnp.array([0, points // 4], jnp.int32).reshape(1, 2, 1)
    lanes = min(128, period)
    blocks = period // lanes
    scale = 2.0 * math.pi / points
    hi_turns = (modes[..., None] * (lax.iota(jnp.int32, blocks) * lanes) + quarter[..., None]) % points
    lo_turns = (modes[..., None] * lax.iota(jnp.int32, lanes)) % points
    hi_angle = hi_turns.astype(jnp.float32) * scale
    lo_angle = lo_turns.astype(jnp.float32) * scale
    ca, sa = jnp.cos(hi_angle)[..., None], jnp.sin(hi_angle)[..., None]
    cb, sb = jnp.cos(lo_angle)[..., None, :], jnp.sin(lo_angle)[..., None, :]
    basis = (ca * cb - sa * sb).reshape(-1, period)
    fwd = (basis * math.sqrt(2.0 / points)).astype(jnp.bfloat16)
    ratio = math.sqrt(points / (2.0 * total_modes))
    if ratio == 2.0 ** round(math.log2(ratio)):
        fwd = lax.optimization_barrier(fwd)
        inv = fwd
    else:
        inv = (basis * math.sqrt(1.0 / total_modes)).astype(jnp.bfloat16)
        ratio = 1.0

    flat = jnp.transpose(field, (1, 2, 0, 3, 4)).reshape(-1, points)
    summed = flat[:, :period].astype(jnp.float32)
    for n in range(1, points // period):
        summed = summed + flat[:, n * period : (n + 1) * period].astype(jnp.float32)
    high = summed.astype(jnp.bfloat16)
    low = (summed - high.astype(jnp.float32)).astype(jnp.bfloat16)
    rows = jnp.concatenate([high, low], axis=1)
    spec_t = lax.dot_general(
        jnp.concatenate([fwd, fwd], axis=1), rows, (((1,), (1,)), ((), ())),
        preferred_element_type=jnp.float32,
    ).astype(jnp.bfloat16)

    sent = spec_t.reshape(devices, 2 * per_dev, row_count)
    got = lax.all_to_all(sent, ("chan", "lat"), 0, 0, tiled=True)
    got = jnp.transpose(got.reshape(n_chan, n_lat, 2 * per_dev, row_count), (0, 2, 1, 3))
    sign = jnp.array([[1.0, 1.0], [1.0, -1.0]], jnp.float32)
    weight = mix_weight.astype(jnp.float32).reshape(-1, n_chan, chans)
    mix_fold = sign[:, None, None, :, None] * weight[None, :, :, None, :]
    mix_fold = mix_fold.reshape(2 * weight.shape[0], -1).astype(jnp.bfloat16)
    piece = cycles
    folded = pl.pallas_call(
        functools.partial(gather_kernel, piece=piece, per_dev=per_dev, pairs=2 * fields),
        out_shape=jax.ShapeDtypeStruct(
            (per_dev, 2, fields, 2, weight.shape[0], n_lat * cycles), jnp.bfloat16
        ),
        scratch_shapes=[pltpu.VMEM((2 * per_dev, fields, n_chan, 2, chans, n_lat * cycles), jnp.float32)],
        compiler_params=pltpu.CompilerParams(vmem_limit_bytes=48 * 1024 * 1024),
    )(got, mix_fold)

    all_gain = lax.all_gather(spectral_gain, "chan", axis=0, tiled=True)
    gain_par = jnp.transpose(all_gain.reshape(-1, half_deg, 2), (2, 0, 1))
    own_modes = lax.dynamic_slice_in_dim(
        modes.reshape(-1), (chan_index * n_lat + lat_index) * per_dev, per_dev, 0
    )
    rows_x = folded.shape[2] * folded.shape[3] * folded.shape[4]
    gain_rows = jnp.tile(gain_par, (1, rows_x // gain_par.shape[1], 1))
    base = (chan_index * per_dev).astype(jnp.int32).reshape(1)
    back = legendre_stage(
        folded.reshape(per_dev, 2, rows_x, -1), legendre, gain_rows, own_modes, base
    )
    spread = pl.pallas_call(
        functools.partial(scatter_kernel, piece=piece, per_dev=per_dev, fields=fields),
        out_shape=jax.ShapeDtypeStruct((n_chan, 2 * per_dev, n_lat, row_count), jnp.bfloat16),
        compiler_params=pltpu.CompilerParams(vmem_limit_bytes=48 * 1024 * 1024),
    )(back)
    leaving = jnp.transpose(spread, (0, 2, 1, 3)).reshape(devices, 2 * per_dev, row_count)
    returned = lax.all_to_all(leaving, ("chan", "lat"), 0, 0, tiled=True)
    returned = returned.reshape(2 * total_modes, row_count)

    waveform = lax.dot_general(
        returned, inv, (((0,), (0,)), ((), ())), preferred_element_type=jnp.float32
    ) * ratio
    waveform = waveform.reshape(fields, 2, chans, cycles, period)
    block = (1,) + field.shape[1:]
    return pl.pallas_call(
        functools.partial(epilogue_kernel, period=period),
        grid=(chans,),
        in_specs=[
            pl.BlockSpec((fields, 2, 1, cycles, period), lambda c: (0, 0, c, 0, 0)),
            pl.BlockSpec(block, lambda c: (c, 0, 0, 0, 0)),
        ],
        out_specs=pl.BlockSpec(block, lambda c: (c, 0, 0, 0, 0)),
        out_shape=jax.ShapeDtypeStruct(field.shape, field.dtype),
        compiler_params=pltpu.CompilerParams(vmem_limit_bytes=48 * 1024 * 1024),
    )(waveform, field)


def solution(mesh):
    n_lat = mesh.shape["lat"]
    n_chan = mesh.shape["chan"]
    placed = (
        P("chan", None, None, "lat", None),
        P(),
        P("chan", None),
        P(None, "lat", None, None),
        P(),
    )

    def body(field, mix_weight, spectral_gain, legendre, slot_mode):
        return local(field, mix_weight, spectral_gain, legendre, slot_mode, n_lat, n_chan)

    return jax.shard_map(
        body,
        mesh=mesh,
        in_specs=placed,
        out_specs=P("chan", None, None, "lat", None),
        check_vma=False,
    )
```

```python
import functools
import math

import jax
import jax.numpy as jnp
from jax import lax
from jax.experimental import pallas as pl
from jax.experimental.pallas import tpu as pltpu
from jax.sharding import PartitionSpec as P


def block_swap(x, piece):
    group, width = x.shape[1], x.shape[2]
    row = lax.broadcasted_iota(jnp.int32, x.shape, 1)
    blk = lax.broadcasted_iota(jnp.int32, x.shape, 2) // piece
    out = jnp.where(blk == row, x, 0.0)
    for d in range(1, group):
        moved = pltpu.roll(x, (-piece * d) % width, 2)
        moved = jnp.where(blk == row, moved, 0.0)
        out = out + pltpu.roll(moved, d, 1)
    return out


def tiles_of(x, group):
    return jnp.stack(
        [
            x[i * group : (i + 1) * group, j * 128 : (j + 1) * 128]
            for i in range(x.shape[0] // group)
            for j in range(x.shape[1] // 128)
        ]
    )


def gather_kernel(got_ref, mix_ref, out_ref, stage_ref, *, piece, per_dev, pairs):
    n_chan = got_ref.shape[0]
    lat_rows = got_ref.shape[2]
    group = 128 // piece

    def one(qs, carry):
        for c in range(n_chan):
            swapped = block_swap(tiles_of(got_ref[c, qs].astype(jnp.float32), group), piece)
            for tile in range(lat_rows // group):
                for th in range(pairs):
                    stage_ref[qs, th // 2, c, th % 2, :, tile * 128 : (tile + 1) * 128] = swapped[
                        tile * pairs + th
                    ]
        q = qs // per_dev
        s = qs % per_dev
        for t in range(pairs // 2):
            block = stage_ref[qs, t]
            block = block.reshape(-1, block.shape[-1]).astype(jnp.bfloat16)
            mixed = jnp.dot(mix_ref[...], block, preferred_element_type=jnp.float32)
            half = mixed.shape[0] // 2
            for p in range(2):
                out_ref[s, p, t, q] = mixed[p * half : (p + 1) * half].astype(out_ref.dtype)
        return carry

    lax.fori_loop(0, got_ref.shape[1], one, 0)


def scatter_kernel(back_ref, out_ref, *, piece, per_dev, fields):
    n_chan = out_ref.shape[0]
    lat_rows = out_ref.shape[2]
    group = 128 // piece
    chans = back_ref.shape[2] // (fields * 2)

    def one(qs, carry):
        q = qs // per_dev
        s = qs % per_dev
        for t in range(fields):
            for h in range(2):
                start = (t * 2 + q) * chans
                part = back_ref[s, h, pl.ds(pl.multiple_of(start, 8), chans)].astype(jnp.float32)
                swapped = block_swap(tiles_of(part, group), piece)
                th = t * 2 + h
                lane_tiles = part.shape[1] // 128
                for c in range(n_chan):
                    column = jnp.concatenate(
                        [swapped[c * lane_tiles + tile] for tile in range(lat_rows // group)], axis=0
                    )
                    out_ref[c, qs, :, th * 128 : (th + 1) * 128] = column.astype(out_ref.dtype)
        return carry

    lax.fori_loop(0, out_ref.shape[1], one, 0)


def epilogue_kernel(wave_ref, field_ref, out_ref, *, period):
    fields = wave_ref.shape[0]
    primal_h = wave_ref[0, :, 0]
    sigmoid_h = 1.0 / (1.0 + jnp.exp(-primal_h))
    slope_h = sigmoid_h * (1.0 + primal_h * (1.0 - sigmoid_h))
    gain_h = primal_h * sigmoid_h
    for n in range(field_ref.shape[-1] // period):
        cols = slice(n * period, (n + 1) * period)
        out_ref[0, 0, :, :, cols] = (
            field_ref[0, 0, :, :, cols].astype(jnp.float32) + gain_h
        ).astype(out_ref.dtype)
        for t in range(1, fields):
            out_ref[0, t, :, :, cols] = (
                field_ref[0, t, :, :, cols].astype(jnp.float32) + slope_h * wave_ref[t, :, 0]
            ).astype(out_ref.dtype)


def legendre_kernel(modes_ref, base_ref, folded_ref, leg_ref, gain_ref, out_ref, *, block):
    s = pl.program_id(0)
    mode = modes_ref[s]
    half_deg = leg_ref.shape[-1]
    rows = folded_ref.shape[-2]
    north = folded_ref.shape[-1]
    syn = []
    for p in range(2):
        lhs = folded_ref[0, p]
        acc = jnp.zeros((rows, north), jnp.float32)
        for b in range(half_deg // block):
            def step(acc, p=p, b=b):
                table = leg_ref[p, 0, :, b * block : (b + 1) * block]
                coef = jnp.dot(lhs, table, preferred_element_type=jnp.float32)
                degree = 2 * (b * block + lax.broadcasted_iota(jnp.int32, (1, block), 1)) + p
                kept = jnp.where(
                    degree >= mode, gain_ref[p, :, b * block : (b + 1) * block] * coef, 0.0
                ).astype(jnp.bfloat16)
                return acc + lax.dot_general(
                    kept, table, (((1,), (1,)), ((), ())), preferred_element_type=jnp.float32
                )
            top = 2 * ((b + 1) * block - 1) + p
            acc = lax.cond(top >= mode, step, lambda a: a, acc)
        syn.append(acc)
    out_ref[0, 0] = (syn[0] + syn[1]).astype(out_ref.dtype)
    out_ref[0, 1] = (syn[0] - syn[1]).astype(out_ref.dtype)


def legendre_stage(folded, legendre, gain_rows, own_modes, base, block=1024):
    per_dev, _, rows, north = folded.shape
    half_deg = legendre.shape[-1]
    grid_spec = pltpu.PrefetchScalarGridSpec(
        num_scalar_prefetch=2,
        grid=(per_dev,),
        in_specs=[
            pl.BlockSpec((1, 2, rows, north), lambda s, m, b: (s, 0, 0, 0)),
            pl.BlockSpec((2, 1, north, half_deg), lambda s, m, b: (0, b[0] + s, 0, 0)),
            pl.BlockSpec((2, rows, half_deg), lambda s, m, b: (0, 0, 0)),
        ],
        out_specs=pl.BlockSpec((1, 2, rows, north), lambda s, m, b: (s, 0, 0, 0)),
    )
    flops = 8 * per_dev * rows * north * half_deg
    return pl.pallas_call(
        functools.partial(legendre_kernel, block=block),
        grid_spec=grid_spec,
        out_shape=jax.ShapeDtypeStruct((per_dev, 2, rows, north), jnp.bfloat16),
        compiler_params=pltpu.CompilerParams(vmem_limit_bytes=48 * 1024 * 1024),
        cost_estimate=pl.CostEstimate(
            flops=flops, transcendentals=0,
            bytes_accessed=2 * per_dev * north * half_deg * 2 + 4 * folded.size + 4 * gain_rows.size,
        ),
    )(own_modes, base, folded, legendre, gain_rows)


def local(field, mix_weight, spectral_gain, legendre, slot_mode, n_lat, n_chan):
    chans = field.shape[0]
    fields = field.shape[1]
    cycles = field.shape[3]
    points = field.shape[4]
    total_modes = slot_mode.shape[0]
    degrees = spectral_gain.shape[1]
    half_deg = degrees // 2
    step_size = degrees // total_modes
    period = points // math.gcd(points, step_size)
    devices = n_lat * n_chan
    per_dev = total_modes // devices
    lat_index = lax.axis_index("lat")
    chan_index = lax.axis_index("chan")
    row_count = chans * fields * 2 * cycles

    modes = (slot_mode * step_size).reshape(n_lat, n_chan, per_dev)
    modes = jnp.transpose(modes, (1, 0, 2)).reshape(devices, 1, per_dev)
    quarter = jnp.array([0, points // 4], jnp.int32).reshape(1, 2, 1)
    lanes = min(128, period)
    blocks = period // lanes
    scale = 2.0 * math.pi / points
    hi_turns = (modes[..., None] * (lax.iota(jnp.int32, blocks) * lanes) + quarter[..., None]) % points
    lo_turns = (modes[..., None] * lax.iota(jnp.int32, lanes)) % points
    hi_angle = hi_turns.astype(jnp.float32) * scale
    lo_angle = lo_turns.astype(jnp.float32) * scale
    ca, sa = jnp.cos(hi_angle)[..., None], jnp.sin(hi_angle)[..., None]
    cb, sb = jnp.cos(lo_angle)[..., None, :], jnp.sin(lo_angle)[..., None, :]
    basis = (ca * cb - sa * sb).reshape(-1, period)
    fwd = (basis * math.sqrt(2.0 / points)).astype(jnp.bfloat16)
    ratio = math.sqrt(points / (2.0 * total_modes))
    if ratio == 2.0 ** round(math.log2(ratio)):
        fwd = lax.optimization_barrier(fwd)
        inv = fwd
    else:
        inv = (basis * math.sqrt(1.0 / total_modes)).astype(jnp.bfloat16)
        ratio = 1.0

    all_gain = lax.all_gather(spectral_gain, "chan", axis=0, tiled=True)
    all_gain, field = lax.optimization_barrier((all_gain, field))
    flat = jnp.transpose(field, (1, 2, 0, 3, 4)).reshape(-1, points)
    summed = flat[:, :period].astype(jnp.float32)
    for n in range(1, points // period):
        summed = summed + flat[:, n * period : (n + 1) * period].astype(jnp.float32)
    high = summed.astype(jnp.bfloat16)
    low = (summed - high.astype(jnp.float32)).astype(jnp.bfloat16)
    rows = jnp.concatenate([high, low], axis=1)
    spec_t = lax.dot_general(
        jnp.concatenate([fwd, fwd], axis=1), rows, (((1,), (1,)), ((), ())),
        preferred_element_type=jnp.float32,
    ).astype(jnp.bfloat16)

    sent = spec_t.reshape(devices, 2 * per_dev, row_count)
    got = lax.all_to_all(sent, ("chan", "lat"), 0, 0, tiled=True)
    got = jnp.transpose(got.reshape(n_chan, n_lat, 2 * per_dev, row_count), (0, 2, 1, 3))
    sign = jnp.array([[1.0, 1.0], [1.0, -1.0]], jnp.float32)
    weight = mix_weight.astype(jnp.float32).reshape(-1, n_chan, chans)
    mix_fold = sign[:, None, None, :, None] * weight[None, :, :, None, :]
    mix_fold = mix_fold.reshape(2 * weight.shape[0], -1).astype(jnp.bfloat16)
    piece = cycles
    folded = pl.pallas_call(
        functools.partial(gather_kernel, piece=piece, per_dev=per_dev, pairs=2 * fields),
        out_shape=jax.ShapeDtypeStruct(
            (per_dev, 2, fields, 2, weight.shape[0], n_lat * cycles), jnp.bfloat16
        ),
        scratch_shapes=[pltpu.VMEM((2 * per_dev, fields, n_chan, 2, chans, n_lat * cycles), jnp.float32)],
        compiler_params=pltpu.CompilerParams(vmem_limit_bytes=48 * 1024 * 1024),
    )(got, mix_fold)

    gain_par = jnp.transpose(all_gain.reshape(-1, half_deg, 2), (2, 0, 1))
    own_modes = lax.dynamic_slice_in_dim(
        modes.reshape(-1), (chan_index * n_lat + lat_index) * per_dev, per_dev, 0
    )
    rows_x = folded.shape[2] * folded.shape[3] * folded.shape[4]
    gain_rows = jnp.tile(gain_par, (1, rows_x // gain_par.shape[1], 1))
    base = (chan_index * per_dev).astype(jnp.int32).reshape(1)
    back = legendre_stage(
        folded.reshape(per_dev, 2, rows_x, -1), legendre, gain_rows, own_modes, base
    )
    spread = pl.pallas_call(
        functools.partial(scatter_kernel, piece=piece, per_dev=per_dev, fields=fields),
        out_shape=jax.ShapeDtypeStruct((n_chan, 2 * per_dev, n_lat, row_count), jnp.bfloat16),
        compiler_params=pltpu.CompilerParams(vmem_limit_bytes=48 * 1024 * 1024),
    )(back)
    leaving = jnp.transpose(spread, (0, 2, 1, 3)).reshape(devices, 2 * per_dev, row_count)
    returned = lax.all_to_all(leaving, ("chan", "lat"), 0, 0, tiled=True)
    returned = returned.reshape(2 * total_modes, row_count)

    waveform = lax.dot_general(
        returned, inv, (((0,), (0,)), ((), ())), preferred_element_type=jnp.float32
    ) * ratio
    waveform = waveform.reshape(fields, 2, chans, cycles, period)
    block = (1,) + field.shape[1:]
    return pl.pallas_call(
        functools.partial(epilogue_kernel, period=period),
        grid=(chans,),
        in_specs=[
            pl.BlockSpec((fields, 2, 1, cycles, period), lambda c: (0, 0, c, 0, 0)),
            pl.BlockSpec(block, lambda c: (c, 0, 0, 0, 0)),
        ],
        out_specs=pl.BlockSpec(block, lambda c: (c, 0, 0, 0, 0)),
        out_shape=jax.ShapeDtypeStruct(field.shape, field.dtype),
        compiler_params=pltpu.CompilerParams(vmem_limit_bytes=48 * 1024 * 1024),
    )(waveform, field)


def solution(mesh):
    n_lat = mesh.shape["lat"]
    n_chan = mesh.shape["chan"]
    placed = (
        P("chan", None, None, "lat", None),
        P(),
        P("chan", None),
        P(None, "lat", None, None),
        P(),
    )

    def body(field, mix_weight, spectral_gain, legendre, slot_mode):
        return local(field, mix_weight, spectral_gain, legendre, slot_mode, n_lat, n_chan)

    return jax.shard_map(
        body,
        mesh=mesh,
        in_specs=placed,
        out_specs=P("chan", None, None, "lat", None),
        check_vma=False,
    )
```

```python
import functools
import math

import jax
import jax.numpy as jnp
from jax import lax
from jax.experimental import pallas as pl
from jax.experimental.pallas import tpu as pltpu
from jax.sharding import PartitionSpec as P


def block_swap(x, piece):
    group, width = x.shape[1], x.shape[2]
    row = lax.broadcasted_iota(jnp.int32, x.shape, 1)
    blk = lax.broadcasted_iota(jnp.int32, x.shape, 2) // piece
    out = jnp.where(blk == row, x, 0.0)
    for d in range(1, group):
        moved = pltpu.roll(x, (-piece * d) % width, 2)
        moved = jnp.where(blk == row, moved, 0.0)
        out = out + pltpu.roll(moved, d, 1)
    return out


def tiles_of(x, group):
    return jnp.stack(
        [
            x[i * group : (i + 1) * group, j * 128 : (j + 1) * 128]
            for i in range(x.shape[0] // group)
            for j in range(x.shape[1] // 128)
        ]
    )


def gather_kernel(got_ref, mix_ref, out_ref, stage_ref, *, piece, per_dev, pairs):
    n_chan = got_ref.shape[0]
    lat_rows = got_ref.shape[2]
    group = 128 // piece

    def one(qs, carry):
        for c in range(n_chan):
            swapped = block_swap(tiles_of(got_ref[c, qs].astype(jnp.float32), group), piece)
            for tile in range(lat_rows // group):
                for th in range(pairs):
                    stage_ref[qs, th // 2, c, th % 2, :, tile * 128 : (tile + 1) * 128] = swapped[
                        tile * pairs + th
                    ]
        q = qs // per_dev
        s = qs % per_dev
        for t in range(pairs // 2):
            block = stage_ref[qs, t]
            block = block.reshape(-1, block.shape[-1]).astype(jnp.bfloat16)
            mixed = jnp.dot(mix_ref[...], block, preferred_element_type=jnp.float32)
            half = mixed.shape[0] // 2
            for p in range(2):
                out_ref[s, p, t, q] = mixed[p * half : (p + 1) * half].astype(out_ref.dtype)
        return carry

    lax.fori_loop(0, got_ref.shape[1], one, 0)


def scatter_kernel(back_ref, out_ref, *, piece, per_dev, fields):
    n_chan = out_ref.shape[0]
    lat_rows = out_ref.shape[2]
    group = 128 // piece
    chans = back_ref.shape[2] // (fields * 2)

    def one(qs, carry):
        q = qs // per_dev
        s = qs % per_dev
        for t in range(fields):
            for h in range(2):
                start = (t * 2 + q) * chans
                part = back_ref[s, h, pl.ds(pl.multiple_of(start, 8), chans)].astype(jnp.float32)
                swapped = block_swap(tiles_of(part, group), piece)
                th = t * 2 + h
                lane_tiles = part.shape[1] // 128
                for c in range(n_chan):
                    column = jnp.concatenate(
                        [swapped[c * lane_tiles + tile] for tile in range(lat_rows // group)], axis=0
                    )
                    out_ref[c, qs, :, th * 128 : (th + 1) * 128] = column.astype(out_ref.dtype)
        return carry

    lax.fori_loop(0, out_ref.shape[1], one, 0)


def epilogue_kernel(wave_ref, field_ref, out_ref, *, period):
    fields = wave_ref.shape[0]
    for c in range(field_ref.shape[0]):
        primal_h = wave_ref[0, :, c]
        sigmoid_h = 1.0 / (1.0 + jnp.exp(-primal_h))
        slope_h = sigmoid_h * (1.0 + primal_h * (1.0 - sigmoid_h))
        gain_h = primal_h * sigmoid_h
        for n in range(field_ref.shape[-1] // period):
            cols = slice(n * period, (n + 1) * period)
            out_ref[c, 0, :, :, cols] = (
                field_ref[c, 0, :, :, cols].astype(jnp.float32) + gain_h
            ).astype(out_ref.dtype)
            for t in range(1, fields):
                out_ref[c, t, :, :, cols] = (
                    field_ref[c, t, :, :, cols].astype(jnp.float32) + slope_h * wave_ref[t, :, c]
                ).astype(out_ref.dtype)


def legendre_kernel(modes_ref, base_ref, folded_ref, leg_ref, gain_ref, out_ref, *, block):
    s = pl.program_id(0)
    mode = modes_ref[s]
    half_deg = leg_ref.shape[-1]
    rows = folded_ref.shape[-2]
    north = folded_ref.shape[-1]
    syn = []
    for p in range(2):
        lhs = folded_ref[0, p]
        acc = jnp.zeros((rows, north), jnp.float32)
        for b in range(half_deg // block):
            def step(acc, p=p, b=b):
                table = leg_ref[p, 0, :, b * block : (b + 1) * block]
                coef = jnp.dot(lhs, table, preferred_element_type=jnp.float32)
                degree = 2 * (b * block + lax.broadcasted_iota(jnp.int32, (1, block), 1)) + p
                kept = jnp.where(
                    degree >= mode, gain_ref[p, :, b * block : (b + 1) * block] * coef, 0.0
                ).astype(jnp.bfloat16)
                return acc + lax.dot_general(
                    kept, table, (((1,), (1,)), ((), ())), preferred_element_type=jnp.float32
                )
            top = 2 * ((b + 1) * block - 1) + p
            acc = lax.cond(top >= mode, step, lambda a: a, acc)
        syn.append(acc)
    out_ref[0, 0] = (syn[0] + syn[1]).astype(out_ref.dtype)
    out_ref[0, 1] = (syn[0] - syn[1]).astype(out_ref.dtype)


def legendre_stage(folded, legendre, gain_rows, own_modes, base, block=1024):
    per_dev, _, rows, north = folded.shape
    half_deg = legendre.shape[-1]
    grid_spec = pltpu.PrefetchScalarGridSpec(
        num_scalar_prefetch=2,
        grid=(per_dev,),
        in_specs=[
            pl.BlockSpec((1, 2, rows, north), lambda s, m, b: (s, 0, 0, 0)),
            pl.BlockSpec((2, 1, north, half_deg), lambda s, m, b: (0, b[0] + s, 0, 0)),
            pl.BlockSpec((2, rows, half_deg), lambda s, m, b: (0, 0, 0)),
        ],
        out_specs=pl.BlockSpec((1, 2, rows, north), lambda s, m, b: (s, 0, 0, 0)),
    )
    flops = 8 * per_dev * rows * north * half_deg
    return pl.pallas_call(
        functools.partial(legendre_kernel, block=block),
        grid_spec=grid_spec,
        out_shape=jax.ShapeDtypeStruct((per_dev, 2, rows, north), jnp.bfloat16),
        compiler_params=pltpu.CompilerParams(vmem_limit_bytes=48 * 1024 * 1024),
        cost_estimate=pl.CostEstimate(
            flops=flops, transcendentals=0,
            bytes_accessed=2 * per_dev * north * half_deg * 2 + 4 * folded.size + 4 * gain_rows.size,
        ),
    )(own_modes, base, folded, legendre, gain_rows)


def local(field, mix_weight, spectral_gain, legendre, slot_mode, n_lat, n_chan):
    chans = field.shape[0]
    fields = field.shape[1]
    cycles = field.shape[3]
    points = field.shape[4]
    total_modes = slot_mode.shape[0]
    degrees = spectral_gain.shape[1]
    half_deg = degrees // 2
    step_size = degrees // total_modes
    period = points // math.gcd(points, step_size)
    devices = n_lat * n_chan
    per_dev = total_modes // devices
    lat_index = lax.axis_index("lat")
    chan_index = lax.axis_index("chan")
    row_count = chans * fields * 2 * cycles

    modes = (slot_mode * step_size).reshape(n_lat, n_chan, per_dev)
    modes = jnp.transpose(modes, (1, 0, 2)).reshape(devices, 1, per_dev)
    quarter = jnp.array([0, points // 4], jnp.int32).reshape(1, 2, 1)
    lanes = min(128, period)
    blocks = period // lanes
    scale = 2.0 * math.pi / points
    hi_turns = (modes[..., None] * (lax.iota(jnp.int32, blocks) * lanes) + quarter[..., None]) % points
    lo_turns = (modes[..., None] * lax.iota(jnp.int32, lanes)) % points
    hi_angle = hi_turns.astype(jnp.float32) * scale
    lo_angle = lo_turns.astype(jnp.float32) * scale
    ca, sa = jnp.cos(hi_angle)[..., None], jnp.sin(hi_angle)[..., None]
    cb, sb = jnp.cos(lo_angle)[..., None, :], jnp.sin(lo_angle)[..., None, :]
    basis = (ca * cb - sa * sb).reshape(-1, period)
    fwd = (basis * math.sqrt(2.0 / points)).astype(jnp.bfloat16)
    ratio = math.sqrt(points / (2.0 * total_modes))
    if ratio == 2.0 ** round(math.log2(ratio)):
        fwd = lax.optimization_barrier(fwd)
        inv = fwd
    else:
        inv = (basis * math.sqrt(1.0 / total_modes)).astype(jnp.bfloat16)
        ratio = 1.0

    flat = jnp.transpose(field, (1, 2, 0, 3, 4)).reshape(-1, points)
    summed = flat[:, :period].astype(jnp.float32)
    for n in range(1, points // period):
        summed = summed + flat[:, n * period : (n + 1) * period].astype(jnp.float32)
    high = summed.astype(jnp.bfloat16)
    low = (summed - high.astype(jnp.float32)).astype(jnp.bfloat16)
    rows = jnp.concatenate([high, low], axis=1)
    spec_t = lax.dot_general(
        jnp.concatenate([fwd, fwd], axis=1), rows, (((1,), (1,)), ((), ())),
        preferred_element_type=jnp.float32,
    ).astype(jnp.bfloat16)

    sent = spec_t.reshape(devices, 2 * per_dev, row_count)
    got = lax.all_to_all(sent, ("chan", "lat"), 0, 0, tiled=True)
    got = jnp.transpose(got.reshape(n_chan, n_lat, 2 * per_dev, row_count), (0, 2, 1, 3))
    sign = jnp.array([[1.0, 1.0], [1.0, -1.0]], jnp.float32)
    weight = mix_weight.astype(jnp.float32).reshape(-1, n_chan, chans)
    mix_fold = sign[:, None, None, :, None] * weight[None, :, :, None, :]
    mix_fold = mix_fold.reshape(2 * weight.shape[0], -1).astype(jnp.bfloat16)
    piece = cycles
    folded = pl.pallas_call(
        functools.partial(gather_kernel, piece=piece, per_dev=per_dev, pairs=2 * fields),
        out_shape=jax.ShapeDtypeStruct(
            (per_dev, 2, fields, 2, weight.shape[0], n_lat * cycles), jnp.bfloat16
        ),
        scratch_shapes=[pltpu.VMEM((2 * per_dev, fields, n_chan, 2, chans, n_lat * cycles), jnp.float32)],
        compiler_params=pltpu.CompilerParams(vmem_limit_bytes=48 * 1024 * 1024),
    )(got, mix_fold)

    all_gain = lax.all_gather(spectral_gain, "chan", axis=0, tiled=True)
    gain_par = jnp.transpose(all_gain.reshape(-1, half_deg, 2), (2, 0, 1))
    own_modes = lax.dynamic_slice_in_dim(
        modes.reshape(-1), (chan_index * n_lat + lat_index) * per_dev, per_dev, 0
    )
    rows_x = folded.shape[2] * folded.shape[3] * folded.shape[4]
    gain_rows = jnp.tile(gain_par, (1, rows_x // gain_par.shape[1], 1))
    base = (chan_index * per_dev).astype(jnp.int32).reshape(1)
    back = legendre_stage(
        folded.reshape(per_dev, 2, rows_x, -1), legendre, gain_rows, own_modes, base
    )
    spread = pl.pallas_call(
        functools.partial(scatter_kernel, piece=piece, per_dev=per_dev, fields=fields),
        out_shape=jax.ShapeDtypeStruct((n_chan, 2 * per_dev, n_lat, row_count), jnp.bfloat16),
        compiler_params=pltpu.CompilerParams(vmem_limit_bytes=48 * 1024 * 1024),
    )(back)
    leaving = jnp.transpose(spread, (0, 2, 1, 3)).reshape(devices, 2 * per_dev, row_count)
    returned = lax.all_to_all(leaving, ("chan", "lat"), 0, 0, tiled=True)
    returned = returned.reshape(2 * total_modes, row_count)

    waveform = lax.dot_general(
        returned, inv, (((0,), (0,)), ((), ())), preferred_element_type=jnp.float32
    ) * ratio
    waveform = waveform.reshape(fields, 2, chans, cycles, period)
    per_step = 2 if chans % 2 == 0 else 1
    block = (per_step,) + field.shape[1:]
    return pl.pallas_call(
        functools.partial(epilogue_kernel, period=period),
        grid=(chans // per_step,),
        in_specs=[
            pl.BlockSpec((fields, 2, per_step, cycles, period), lambda c: (0, 0, c, 0, 0)),
            pl.BlockSpec(block, lambda c: (c, 0, 0, 0, 0)),
        ],
        out_specs=pl.BlockSpec(block, lambda c: (c, 0, 0, 0, 0)),
        out_shape=jax.ShapeDtypeStruct(field.shape, field.dtype),
        compiler_params=pltpu.CompilerParams(vmem_limit_bytes=48 * 1024 * 1024),
    )(waveform, field)


def solution(mesh):
    n_lat = mesh.shape["lat"]
    n_chan = mesh.shape["chan"]
    placed = (
        P("chan", None, None, "lat", None),
        P(),
        P("chan", None),
        P(None, "lat", None, None),
        P(),
    )

    def body(field, mix_weight, spectral_gain, legendre, slot_mode):
        return local(field, mix_weight, spectral_gain, legendre, slot_mode, n_lat, n_chan)

    return jax.shard_map(
        body,
        mesh=mesh,
        in_specs=placed,
        out_specs=P("chan", None, None, "lat", None),
        check_vma=False,
    )
```

```python
import functools
import math

import jax
import jax.numpy as jnp
from jax import lax
from jax.experimental import pallas as pl
from jax.experimental.pallas import tpu as pltpu
from jax.sharding import PartitionSpec as P


def block_swap(x, piece):
    group, width = x.shape[1], x.shape[2]
    row = lax.broadcasted_iota(jnp.int32, x.shape, 1)
    blk = lax.broadcasted_iota(jnp.int32, x.shape, 2) // piece
    out = jnp.where(blk == row, x, 0.0)
    for d in range(1, group):
        moved = pltpu.roll(x, (-piece * d) % width, 2)
        moved = jnp.where(blk == row, moved, 0.0)
        out = out + pltpu.roll(moved, d, 1)
    return out


def tiles_of(x, group):
    return jnp.stack(
        [
            x[i * group : (i + 1) * group, j * 128 : (j + 1) * 128]
            for i in range(x.shape[0] // group)
            for j in range(x.shape[1] // 128)
        ]
    )


def gather_kernel(got_ref, mix_ref, out_ref, stage_ref, *, piece, per_dev, pairs):
    n_chan = got_ref.shape[0]
    lat_rows = got_ref.shape[2]
    group = 128 // piece

    def one(qs, carry):
        for c in range(n_chan):
            swapped = block_swap(tiles_of(got_ref[c, qs].astype(jnp.float32), group), piece)
            for tile in range(lat_rows // group):
                for th in range(pairs):
                    stage_ref[qs, th // 2, c, th % 2, :, tile * 128 : (tile + 1) * 128] = swapped[
                        tile * pairs + th
                    ]
        q = qs // per_dev
        s = qs % per_dev
        for t in range(pairs // 2):
            block = stage_ref[qs, t]
            block = block.reshape(-1, block.shape[-1]).astype(jnp.bfloat16)
            mixed = jnp.dot(mix_ref[...], block, preferred_element_type=jnp.float32)
            half = mixed.shape[0] // 2
            for p in range(2):
                out_ref[s, p, t, q] = mixed[p * half : (p + 1) * half].astype(out_ref.dtype)
        return carry

    lax.fori_loop(0, got_ref.shape[1], one, 0)


def scatter_kernel(back_ref, out_ref, *, piece, per_dev, fields):
    n_chan = out_ref.shape[0]
    lat_rows = out_ref.shape[2]
    group = 128 // piece
    chans = back_ref.shape[2] // (fields * 2)

    def one(qs, carry):
        q = qs // per_dev
        s = qs % per_dev
        for t in range(fields):
            for h in range(2):
                start = (t * 2 + q) * chans
                part = back_ref[s, h, pl.ds(pl.multiple_of(start, 8), chans)].astype(jnp.float32)
                swapped = block_swap(tiles_of(part, group), piece)
                th = t * 2 + h
                lane_tiles = part.shape[1] // 128
                for c in range(n_chan):
                    column = jnp.concatenate(
                        [swapped[c * lane_tiles + tile] for tile in range(lat_rows // group)], axis=0
                    )
                    out_ref[c, qs, :, th * 128 : (th + 1) * 128] = column.astype(out_ref.dtype)
        return carry

    lax.fori_loop(0, out_ref.shape[1], one, 0)


def epilogue_kernel(wave_ref, field_ref, out_ref, *, period):
    fields = wave_ref.shape[0]
    for c in range(field_ref.shape[0]):
        primal_h = wave_ref[0, :, c]
        sigmoid_h = 1.0 / (1.0 + jnp.exp(-primal_h))
        slope_h = sigmoid_h * (1.0 + primal_h * (1.0 - sigmoid_h))
        gain_h = primal_h * sigmoid_h
        for n in range(field_ref.shape[-1] // period):
            cols = slice(n * period, (n + 1) * period)
            out_ref[c, 0, :, :, cols] = (
                field_ref[c, 0, :, :, cols].astype(jnp.float32) + gain_h
            ).astype(out_ref.dtype)
            for t in range(1, fields):
                out_ref[c, t, :, :, cols] = (
                    field_ref[c, t, :, :, cols].astype(jnp.float32) + slope_h * wave_ref[t, :, c]
                ).astype(out_ref.dtype)


def legendre_kernel(modes_ref, base_ref, folded_ref, leg_ref, gain_ref, out_ref, *, block):
    s = pl.program_id(0)
    mode = modes_ref[s]
    half_deg = leg_ref.shape[-1]
    rows = folded_ref.shape[-2]
    north = folded_ref.shape[-1]
    syn = []
    for p in range(2):
        lhs = folded_ref[0, p]
        acc = jnp.zeros((rows, north), jnp.float32)
        for b in range(half_deg // block):
            def step(acc, p=p, b=b):
                table = leg_ref[p, 0, :, b * block : (b + 1) * block]
                coef = jnp.dot(lhs, table, preferred_element_type=jnp.float32)
                degree = 2 * (b * block + lax.broadcasted_iota(jnp.int32, (1, block), 1)) + p
                kept = jnp.where(
                    degree >= mode, gain_ref[p, :, b * block : (b + 1) * block] * coef, 0.0
                ).astype(jnp.bfloat16)
                return acc + lax.dot_general(
                    kept, table, (((1,), (1,)), ((), ())), preferred_element_type=jnp.float32
                )
            top = 2 * ((b + 1) * block - 1) + p
            acc = lax.cond(top >= mode, step, lambda a: a, acc)
        syn.append(acc)
    out_ref[0, 0] = (syn[0] + syn[1]).astype(out_ref.dtype)
    out_ref[0, 1] = (syn[0] - syn[1]).astype(out_ref.dtype)


def legendre_stage(folded, legendre, gain_rows, own_modes, base, block=1024):
    per_dev, _, rows, north = folded.shape
    half_deg = legendre.shape[-1]
    grid_spec = pltpu.PrefetchScalarGridSpec(
        num_scalar_prefetch=2,
        grid=(per_dev,),
        in_specs=[
            pl.BlockSpec((1, 2, rows, north), lambda s, m, b: (s, 0, 0, 0)),
            pl.BlockSpec((2, 1, north, half_deg), lambda s, m, b: (0, b[0] + s, 0, 0)),
            pl.BlockSpec((2, rows, half_deg), lambda s, m, b: (0, 0, 0)),
        ],
        out_specs=pl.BlockSpec((1, 2, rows, north), lambda s, m, b: (s, 0, 0, 0)),
    )
    flops = 8 * per_dev * rows * north * half_deg
    return pl.pallas_call(
        functools.partial(legendre_kernel, block=block),
        grid_spec=grid_spec,
        out_shape=jax.ShapeDtypeStruct((per_dev, 2, rows, north), jnp.bfloat16),
        compiler_params=pltpu.CompilerParams(vmem_limit_bytes=48 * 1024 * 1024),
        cost_estimate=pl.CostEstimate(
            flops=flops, transcendentals=0,
            bytes_accessed=2 * per_dev * north * half_deg * 2 + 4 * folded.size + 4 * gain_rows.size,
        ),
    )(own_modes, base, folded, legendre, gain_rows)


def local(field, mix_weight, spectral_gain, legendre, slot_mode, n_lat, n_chan):
    chans = field.shape[0]
    fields = field.shape[1]
    cycles = field.shape[3]
    points = field.shape[4]
    total_modes = slot_mode.shape[0]
    degrees = spectral_gain.shape[1]
    half_deg = degrees // 2
    step_size = degrees // total_modes
    period = points // math.gcd(points, step_size)
    devices = n_lat * n_chan
    per_dev = total_modes // devices
    lat_index = lax.axis_index("lat")
    chan_index = lax.axis_index("chan")
    row_count = chans * fields * 2 * cycles

    modes = (slot_mode * step_size).reshape(n_lat, n_chan, per_dev)
    modes = jnp.transpose(modes, (1, 0, 2)).reshape(devices, 1, per_dev)
    quarter = jnp.array([0, points // 4], jnp.int32).reshape(1, 2, 1)
    lanes = min(128, period)
    blocks = period // lanes
    scale = 2.0 * math.pi / points
    hi_turns = (modes[..., None] * (lax.iota(jnp.int32, blocks) * lanes) + quarter[..., None]) % points
    lo_turns = (modes[..., None] * lax.iota(jnp.int32, lanes)) % points
    hi_angle = hi_turns.astype(jnp.float32) * scale
    lo_angle = lo_turns.astype(jnp.float32) * scale
    ca, sa = jnp.cos(hi_angle)[..., None], jnp.sin(hi_angle)[..., None]
    cb, sb = jnp.cos(lo_angle)[..., None, :], jnp.sin(lo_angle)[..., None, :]
    basis = (ca * cb - sa * sb).reshape(-1, period)
    fwd = (basis * math.sqrt(2.0 / points)).astype(jnp.bfloat16)
    ratio = math.sqrt(points / (2.0 * total_modes))
    if ratio == 2.0 ** round(math.log2(ratio)):
        fwd = lax.optimization_barrier(fwd)
        inv = fwd
    else:
        inv = (basis * math.sqrt(1.0 / total_modes)).astype(jnp.bfloat16)
        ratio = 1.0

    flat = jnp.transpose(field, (1, 2, 0, 3, 4)).reshape(-1, points)
    summed = flat[:, :period].astype(jnp.float32)
    for n in range(1, points // period):
        summed = summed + flat[:, n * period : (n + 1) * period].astype(jnp.float32)
    high = summed.astype(jnp.bfloat16)
    low = (summed - high.astype(jnp.float32)).astype(jnp.bfloat16)
    rows = jnp.concatenate([high, low], axis=1)
    spec_t = lax.dot_general(
        jnp.concatenate([fwd, fwd], axis=1), rows, (((1,), (1,)), ((), ())),
        preferred_element_type=jnp.float32,
    ).astype(jnp.bfloat16)

    sent = spec_t.reshape(devices, 2 * per_dev, row_count)
    got = lax.all_to_all(sent, ("chan", "lat"), 0, 0, tiled=True)
    got = jnp.transpose(got.reshape(n_chan, n_lat, 2 * per_dev, row_count), (0, 2, 1, 3))
    sign = jnp.array([[1.0, 1.0], [1.0, -1.0]], jnp.float32)
    weight = mix_weight.astype(jnp.float32).reshape(-1, n_chan, chans)
    mix_fold = sign[:, None, None, :, None] * weight[None, :, :, None, :]
    mix_fold = mix_fold.reshape(2 * weight.shape[0], -1).astype(jnp.bfloat16)
    piece = cycles
    folded = pl.pallas_call(
        functools.partial(gather_kernel, piece=piece, per_dev=per_dev, pairs=2 * fields),
        out_shape=jax.ShapeDtypeStruct(
            (per_dev, 2, fields, 2, weight.shape[0], n_lat * cycles), jnp.bfloat16
        ),
        scratch_shapes=[pltpu.VMEM((2 * per_dev, fields, n_chan, 2, chans, n_lat * cycles), jnp.float32)],
        compiler_params=pltpu.CompilerParams(vmem_limit_bytes=48 * 1024 * 1024),
    )(got, mix_fold)

    all_gain = lax.all_gather(spectral_gain, "chan", axis=0, tiled=True)
    gain_par = jnp.transpose(all_gain.reshape(-1, half_deg, 2), (2, 0, 1))
    own_modes = lax.dynamic_slice_in_dim(
        modes.reshape(-1), (chan_index * n_lat + lat_index) * per_dev, per_dev, 0
    )
    rows_x = folded.shape[2] * folded.shape[3] * folded.shape[4]
    gain_rows = jnp.tile(gain_par, (1, rows_x // gain_par.shape[1], 1))
    base = (chan_index * per_dev).astype(jnp.int32).reshape(1)
    back = legendre_stage(
        folded.reshape(per_dev, 2, rows_x, -1), legendre, gain_rows, own_modes, base
    )
    spread = pl.pallas_call(
        functools.partial(scatter_kernel, piece=piece, per_dev=per_dev, fields=fields),
        out_shape=jax.ShapeDtypeStruct((n_chan, 2 * per_dev, n_lat, row_count), jnp.bfloat16),
        compiler_params=pltpu.CompilerParams(vmem_limit_bytes=48 * 1024 * 1024),
    )(back)
    leaving = jnp.transpose(spread, (0, 2, 1, 3)).reshape(devices, 2 * per_dev, row_count)
    returned = lax.all_to_all(leaving, ("chan", "lat"), 0, 0, tiled=True)
    returned = returned.reshape(2 * total_modes, row_count)

    waveform = lax.dot_general(
        returned, inv, (((0,), (0,)), ((), ())), preferred_element_type=jnp.float32
    ) * ratio
    waveform = waveform.reshape(fields, 2, chans, cycles, period)
    per_step = 4 if chans % 4 == 0 else 1
    block = (per_step,) + field.shape[1:]
    return pl.pallas_call(
        functools.partial(epilogue_kernel, period=period),
        grid=(chans // per_step,),
        in_specs=[
            pl.BlockSpec((fields, 2, per_step, cycles, period), lambda c: (0, 0, c, 0, 0)),
            pl.BlockSpec(block, lambda c: (c, 0, 0, 0, 0)),
        ],
        out_specs=pl.BlockSpec(block, lambda c: (c, 0, 0, 0, 0)),
        out_shape=jax.ShapeDtypeStruct(field.shape, field.dtype),
        compiler_params=pltpu.CompilerParams(vmem_limit_bytes=48 * 1024 * 1024),
    )(waveform, field)


def solution(mesh):
    n_lat = mesh.shape["lat"]
    n_chan = mesh.shape["chan"]
    placed = (
        P("chan", None, None, "lat", None),
        P(),
        P("chan", None),
        P(None, "lat", None, None),
        P(),
    )

    def body(field, mix_weight, spectral_gain, legendre, slot_mode):
        return local(field, mix_weight, spectral_gain, legendre, slot_mode, n_lat, n_chan)

    return jax.shard_map(
        body,
        mesh=mesh,
        in_specs=placed,
        out_specs=P("chan", None, None, "lat", None),
        check_vma=False,
    )
```

```python
import functools
import math

import jax
import jax.numpy as jnp
from jax import lax
from jax.experimental import pallas as pl
from jax.experimental.pallas import tpu as pltpu
from jax.sharding import PartitionSpec as P


def block_swap(x, piece):
    group, width = x.shape[1], x.shape[2]
    row = lax.broadcasted_iota(jnp.int32, x.shape, 1)
    blk = lax.broadcasted_iota(jnp.int32, x.shape, 2) // piece
    out = jnp.where(blk == row, x, 0.0)
    for d in range(1, group):
        moved = pltpu.roll(x, (-piece * d) % width, 2)
        moved = jnp.where(blk == row, moved, 0.0)
        out = out + pltpu.roll(moved, d, 1)
    return out


def tiles_of(x, group):
    return jnp.stack(
        [
            x[i * group : (i + 1) * group, j * 128 : (j + 1) * 128]
            for i in range(x.shape[0] // group)
            for j in range(x.shape[1] // 128)
        ]
    )


def gather_kernel(got_ref, mix_ref, out_ref, stage_ref, *, piece, per_dev, pairs):
    n_chan = got_ref.shape[0]
    lat_rows = got_ref.shape[2]
    group = 128 // piece

    def one(qs, carry):
        for c in range(n_chan):
            swapped = block_swap(tiles_of(got_ref[c, qs].astype(jnp.float32), group), piece)
            for tile in range(lat_rows // group):
                for th in range(pairs):
                    stage_ref[qs, th // 2, c, th % 2, :, tile * 128 : (tile + 1) * 128] = swapped[
                        tile * pairs + th
                    ]
        q = qs // per_dev
        s = qs % per_dev
        for t in range(pairs // 2):
            block = stage_ref[qs, t]
            block = block.reshape(-1, block.shape[-1]).astype(jnp.bfloat16)
            mixed = jnp.dot(mix_ref[...], block, preferred_element_type=jnp.float32)
            half = mixed.shape[0] // 2
            for p in range(2):
                out_ref[s, p, t, q] = mixed[p * half : (p + 1) * half].astype(out_ref.dtype)
        return carry

    lax.fori_loop(0, got_ref.shape[1], one, 0)


def scatter_kernel(back_ref, out_ref, *, piece, per_dev, fields):
    n_chan = out_ref.shape[0]
    lat_rows = out_ref.shape[2]
    group = 128 // piece
    chans = back_ref.shape[2] // (fields * 2)

    def one(qs, carry):
        q = qs // per_dev
        s = qs % per_dev
        for t in range(fields):
            for h in range(2):
                start = (t * 2 + q) * chans
                part = back_ref[s, h, pl.ds(pl.multiple_of(start, 8), chans)].astype(jnp.float32)
                swapped = block_swap(tiles_of(part, group), piece)
                th = t * 2 + h
                lane_tiles = part.shape[1] // 128
                for c in range(n_chan):
                    column = jnp.concatenate(
                        [swapped[c * lane_tiles + tile] for tile in range(lat_rows // group)], axis=0
                    )
                    out_ref[c, qs, :, th * 128 : (th + 1) * 128] = column.astype(out_ref.dtype)
        return carry

    lax.fori_loop(0, out_ref.shape[1], one, 0)


def epilogue_kernel(wave_ref, field_ref, out_ref, *, period):
    fields = wave_ref.shape[0]
    for c in range(field_ref.shape[0]):
        primal_h = wave_ref[0, :, c]
        sigmoid_h = 1.0 / (1.0 + jnp.exp(-primal_h))
        slope_h = sigmoid_h * (1.0 + primal_h * (1.0 - sigmoid_h))
        gain_h = primal_h * sigmoid_h
        for n in range(field_ref.shape[-1] // period):
            cols = slice(n * period, (n + 1) * period)
            out_ref[c, 0, :, :, cols] = (
                field_ref[c, 0, :, :, cols].astype(jnp.float32) + gain_h
            ).astype(out_ref.dtype)
            for t in range(1, fields):
                out_ref[c, t, :, :, cols] = (
                    field_ref[c, t, :, :, cols].astype(jnp.float32) + slope_h * wave_ref[t, :, c]
                ).astype(out_ref.dtype)


def legendre_kernel(modes_ref, base_ref, folded_ref, leg_ref, gain_ref, out_ref, *, block):
    s = pl.program_id(0)
    mode = modes_ref[s]
    half_deg = leg_ref.shape[-1]
    rows = folded_ref.shape[-2]
    north = folded_ref.shape[-1]
    syn = []
    for p in range(2):
        lhs = folded_ref[0, p]
        acc = jnp.zeros((rows, north), jnp.float32)
        for b in range(half_deg // block):
            def step(acc, p=p, b=b):
                table = leg_ref[p, 0, :, b * block : (b + 1) * block]
                coef = jnp.dot(lhs, table, preferred_element_type=jnp.float32)
                degree = 2 * (b * block + lax.broadcasted_iota(jnp.int32, (1, block), 1)) + p
                kept = jnp.where(
                    degree >= mode, gain_ref[p, :, b * block : (b + 1) * block] * coef, 0.0
                ).astype(jnp.bfloat16)
                return acc + lax.dot_general(
                    kept, table, (((1,), (1,)), ((), ())), preferred_element_type=jnp.float32
                )
            if half_deg // block == 1:
                acc = step(acc)
            else:
                top = 2 * ((b + 1) * block - 1) + p
                acc = lax.cond(top >= mode, step, lambda a: a, acc)
        syn.append(acc)
    out_ref[0, 0] = (syn[0] + syn[1]).astype(out_ref.dtype)
    out_ref[0, 1] = (syn[0] - syn[1]).astype(out_ref.dtype)


def legendre_stage(folded, legendre, gain_rows, own_modes, base, block=1024):
    per_dev, _, rows, north = folded.shape
    half_deg = legendre.shape[-1]
    grid_spec = pltpu.PrefetchScalarGridSpec(
        num_scalar_prefetch=2,
        grid=(per_dev,),
        in_specs=[
            pl.BlockSpec((1, 2, rows, north), lambda s, m, b: (s, 0, 0, 0)),
            pl.BlockSpec((2, 1, north, half_deg), lambda s, m, b: (0, b[0] + s, 0, 0)),
            pl.BlockSpec((2, rows, half_deg), lambda s, m, b: (0, 0, 0)),
        ],
        out_specs=pl.BlockSpec((1, 2, rows, north), lambda s, m, b: (s, 0, 0, 0)),
    )
    flops = 8 * per_dev * rows * north * half_deg
    return pl.pallas_call(
        functools.partial(legendre_kernel, block=block),
        grid_spec=grid_spec,
        out_shape=jax.ShapeDtypeStruct((per_dev, 2, rows, north), jnp.bfloat16),
        compiler_params=pltpu.CompilerParams(vmem_limit_bytes=48 * 1024 * 1024),
        cost_estimate=pl.CostEstimate(
            flops=flops, transcendentals=0,
            bytes_accessed=2 * per_dev * north * half_deg * 2 + 4 * folded.size + 4 * gain_rows.size,
        ),
    )(own_modes, base, folded, legendre, gain_rows)


def local(field, mix_weight, spectral_gain, legendre, slot_mode, n_lat, n_chan):
    chans = field.shape[0]
    fields = field.shape[1]
    cycles = field.shape[3]
    points = field.shape[4]
    total_modes = slot_mode.shape[0]
    degrees = spectral_gain.shape[1]
    half_deg = degrees // 2
    step_size = degrees // total_modes
    period = points // math.gcd(points, step_size)
    devices = n_lat * n_chan
    per_dev = total_modes // devices
    lat_index = lax.axis_index("lat")
    chan_index = lax.axis_index("chan")
    row_count = chans * fields * 2 * cycles

    modes = (slot_mode * step_size).reshape(n_lat, n_chan, per_dev)
    modes = jnp.transpose(modes, (1, 0, 2)).reshape(devices, 1, per_dev)
    quarter = jnp.array([0, points // 4], jnp.int32).reshape(1, 2, 1)
    lanes = min(128, period)
    blocks = period // lanes
    scale = 2.0 * math.pi / points
    hi_turns = (modes[..., None] * (lax.iota(jnp.int32, blocks) * lanes) + quarter[..., None]) % points
    lo_turns = (modes[..., None] * lax.iota(jnp.int32, lanes)) % points
    hi_angle = hi_turns.astype(jnp.float32) * scale
    lo_angle = lo_turns.astype(jnp.float32) * scale
    ca, sa = jnp.cos(hi_angle)[..., None], jnp.sin(hi_angle)[..., None]
    cb, sb = jnp.cos(lo_angle)[..., None, :], jnp.sin(lo_angle)[..., None, :]
    basis = (ca * cb - sa * sb).reshape(-1, period)
    fwd = (basis * math.sqrt(2.0 / points)).astype(jnp.bfloat16)
    ratio = math.sqrt(points / (2.0 * total_modes))
    if ratio == 2.0 ** round(math.log2(ratio)):
        fwd = lax.optimization_barrier(fwd)
        inv = fwd
    else:
        inv = (basis * math.sqrt(1.0 / total_modes)).astype(jnp.bfloat16)
        ratio = 1.0

    flat = jnp.transpose(field, (1, 2, 0, 3, 4)).reshape(-1, points)
    summed = flat[:, :period].astype(jnp.float32)
    for n in range(1, points // period):
        summed = summed + flat[:, n * period : (n + 1) * period].astype(jnp.float32)
    high = summed.astype(jnp.bfloat16)
    low = (summed - high.astype(jnp.float32)).astype(jnp.bfloat16)
    rows = jnp.concatenate([high, low], axis=1)
    spec_t = lax.dot_general(
        jnp.concatenate([fwd, fwd], axis=1), rows, (((1,), (1,)), ((), ())),
        preferred_element_type=jnp.float32,
    ).astype(jnp.bfloat16)

    sent = spec_t.reshape(devices, 2 * per_dev, row_count)
    got = lax.all_to_all(sent, ("chan", "lat"), 0, 0, tiled=True)
    got = jnp.transpose(got.reshape(n_chan, n_lat, 2 * per_dev, row_count), (0, 2, 1, 3))
    sign = jnp.array([[1.0, 1.0], [1.0, -1.0]], jnp.float32)
    weight = mix_weight.astype(jnp.float32).reshape(-1, n_chan, chans)
    mix_fold = sign[:, None, None, :, None] * weight[None, :, :, None, :]
    mix_fold = mix_fold.reshape(2 * weight.shape[0], -1).astype(jnp.bfloat16)
    piece = cycles
    folded = pl.pallas_call(
        functools.partial(gather_kernel, piece=piece, per_dev=per_dev, pairs=2 * fields),
        out_shape=jax.ShapeDtypeStruct(
            (per_dev, 2, fields, 2, weight.shape[0], n_lat * cycles), jnp.bfloat16
        ),
        scratch_shapes=[pltpu.VMEM((2 * per_dev, fields, n_chan, 2, chans, n_lat * cycles), jnp.float32)],
        compiler_params=pltpu.CompilerParams(vmem_limit_bytes=48 * 1024 * 1024),
    )(got, mix_fold)

    all_gain = lax.all_gather(spectral_gain, "chan", axis=0, tiled=True)
    gain_par = jnp.transpose(all_gain.reshape(-1, half_deg, 2), (2, 0, 1))
    own_modes = lax.dynamic_slice_in_dim(
        modes.reshape(-1), (chan_index * n_lat + lat_index) * per_dev, per_dev, 0
    )
    rows_x = folded.shape[2] * folded.shape[3] * folded.shape[4]
    gain_rows = jnp.tile(gain_par, (1, rows_x // gain_par.shape[1], 1))
    base = (chan_index * per_dev).astype(jnp.int32).reshape(1)
    back = legendre_stage(
        folded.reshape(per_dev, 2, rows_x, -1), legendre, gain_rows, own_modes, base
    )
    spread = pl.pallas_call(
        functools.partial(scatter_kernel, piece=piece, per_dev=per_dev, fields=fields),
        out_shape=jax.ShapeDtypeStruct((n_chan, 2 * per_dev, n_lat, row_count), jnp.bfloat16),
        compiler_params=pltpu.CompilerParams(vmem_limit_bytes=48 * 1024 * 1024),
    )(back)
    leaving = jnp.transpose(spread, (0, 2, 1, 3)).reshape(devices, 2 * per_dev, row_count)
    returned = lax.all_to_all(leaving, ("chan", "lat"), 0, 0, tiled=True)
    returned = returned.reshape(2 * total_modes, row_count)

    waveform = lax.dot_general(
        returned, inv, (((0,), (0,)), ((), ())), preferred_element_type=jnp.float32
    ) * ratio
    waveform = waveform.reshape(fields, 2, chans, cycles, period)
    per_step = 4 if chans % 4 == 0 else 1
    block = (per_step,) + field.shape[1:]
    return pl.pallas_call(
        functools.partial(epilogue_kernel, period=period),
        grid=(chans // per_step,),
        in_specs=[
            pl.BlockSpec((fields, 2, per_step, cycles, period), lambda c: (0, 0, c, 0, 0)),
            pl.BlockSpec(block, lambda c: (c, 0, 0, 0, 0)),
        ],
        out_specs=pl.BlockSpec(block, lambda c: (c, 0, 0, 0, 0)),
        out_shape=jax.ShapeDtypeStruct(field.shape, field.dtype),
        compiler_params=pltpu.CompilerParams(vmem_limit_bytes=48 * 1024 * 1024),
    )(waveform, field)


def solution(mesh):
    n_lat = mesh.shape["lat"]
    n_chan = mesh.shape["chan"]
    placed = (
        P("chan", None, None, "lat", None),
        P(),
        P("chan", None),
        P(None, "lat", None, None),
        P(),
    )

    def body(field, mix_weight, spectral_gain, legendre, slot_mode):
        return local(field, mix_weight, spectral_gain, legendre, slot_mode, n_lat, n_chan)

    return jax.shard_map(
        body,
        mesh=mesh,
        in_specs=placed,
        out_specs=P("chan", None, None, "lat", None),
        check_vma=False,
    )
```
